256 devices in a mesh: req: 64 (over y, z_lo, x, core), tp: 4 (over z_hi).
Axes of the slice: x: 4, y: 4, z: 8 (z_hi: 4, z_lo: 2; z = z_hi * 2 + z_lo), core: 2. Of those that a mesh axis runs over, the one named last changes fastest.
Arguments:
- tokens: bfloat16 [16384, 2048], P('req'), may hold values from -6 to 6
- norm_gain: float32 [2048], replicated, may hold values from 0.25 to 1.75
- w_query: bfloat16 [2048, 2048], P(None, 'tp'), may hold values from -1 to 1
- w_key: bfloat16 [2048, 2048], P(None, 'tp'), may hold values from -1 to 1
- w_value: bfloat16 [2048, 2048], P(None, 'tp'), may hold values from -0.125 to 0.125
- w_out: bfloat16 [2048, 2048], P('tp'), may hold values from -0.125 to 0.125
- lambdas: float32 [4, 8, 128], P(None, 'tp'), may hold values from -1 to 1
- sub_gain: float32 [8, 256], P('tp'), may hold values from 0.5 to 2
- lengths: int32 [4], replicated, may hold values from 1 to 8192, 16384 in all
Outputs:
- hidden: bfloat16 [16384, 2048], P('req')
- key_cache: bfloat16 [16384, 2048], P('req', 'tp')
- value_cache: bfloat16 [16384, 2048], P('req', 'tp')
The draws below stay inside these ranges and needn't reach their ends.
Inputs may be any that keep to these rules, and one draw needn't show every extreme that they name: The lengths sum to 16384; the longest is exactly 8192.
All inputs are finite; a program needn't handle non-finite values.
Results may differ from the reference program's by a relative error of at most 0.007.
Values may be sent and summed in bfloat16 or wider, within the bound.
No kernel may reach another device: no remote copies, remote signals or barrier semaphores. Data moves between devices by JAX's collectives and lax.ppermute only.
A program may use at most 128 MiB of HBM per device.

```python
import math
import jax
import jax.numpy as jnp
import numpy as np
from jax import lax

D = 2048
HEADS = 8
QK = 128
VD = 256
TOK_DEV = 256
NPROMPTS = 4
TOKENS = 16384
MAXLEN = 8192


def paired_weights(key):
    base = jax.random.fold_in(key, 7)
    cols = HEADS * 2 * QK
    query = jax.random.truncated_normal(jax.random.fold_in(base, 4), -6.0, 6.0, (D, cols), jnp.float32) * D ** (-0.5)
    keys = jax.random.truncated_normal(jax.random.fold_in(base, 5), -6.0, 6.0, (D, cols), jnp.float32) * D ** (-0.5)
    return (query, keys)


def draw_w_query(key, part):
    return paired_weights(key)[0].astype(jnp.bfloat16)


def draw_w_key(key, part):
    return paired_weights(key)[1].astype(jnp.bfloat16)


def draw_lambdas(key, part):
    base = jax.random.fold_in(key, 11)
    unit = QK ** (-0.5)
    flips = jnp.where(jax.random.bernoulli(jax.random.fold_in(base, 1), 0.5, (HEADS, 1)), 1.0, -1.0).astype(jnp.float32)
    first = jax.random.uniform(jax.random.fold_in(base, 2), (HEADS, QK), jnp.float32, 0.7, 1.3) * unit * flips
    second = jax.random.uniform(jax.random.fold_in(base, 3), (HEADS, QK), jnp.float32, 0.7, 1.3) * unit
    third = jax.random.uniform(jax.random.fold_in(base, 4), (HEADS, QK), jnp.float32, -0.3, 0.3) * unit
    fourth = jax.random.uniform(jax.random.fold_in(base, 5), (HEADS, QK), jnp.float32, -0.3, 0.3) * unit
    return jnp.stack([first, second, third, fourth], axis=0)


def shard_levels(own_key, extent, pieces, smallest, largest):
    level, own = 1.0, jax.random.fold_in(own_key, 6)
    for dim, blocks in pieces:
        draws = jnp.exp(jax.random.uniform(jax.random.fold_in(own, dim), (blocks,), jnp.float32, smallest / len(pieces), largest / len(pieces)))
        level = level * jnp.repeat(draws, extent[dim] // blocks).reshape([-1 if axis == dim else 1 for axis in range(len(extent))])
    return level


def split_up(count, total, bound, slope):
    loads = [(1 << 20) // math.isqrt(grade ** slope) + 1 for grade in range(2, count + 1)]
    surplus, counts = total - bound - (count - 1), [1] * (count - 1)
    while surplus > 0:
        free = [i for i in range(count - 1) if counts[i] < bound]
        whole, left = sum([loads[i] for i in free]), surplus
        for i in free:
            addition = min(bound - counts[i], max(1, left * loads[i] // whole), surplus)
            counts[i] = counts[i] + addition
            surplus = surplus - addition
    return np.array([bound] + counts)


def ragged(own_key, amount, total, reach, skew):
    if amount == 2:
        one = jax.random.randint(own_key, (), max(1, total - reach), min(reach, total - 1) + 1)
        return jnp.stack([one, total - one])
    sizes = jnp.asarray(split_up(amount, total, reach, skew), jnp.int32)
    pairs = (amount - 1) // 2
    donor, receiver = sizes[1:1 + 2 * pairs:2], sizes[2:2 + 2 * pairs:2]
    room = jnp.minimum(donor - 1, reach - receiver)
    moved = jax.random.randint(jax.random.fold_in(own_key, 1), (pairs,), 0, 1 << 20) % (room + 1)
    sizes = sizes.at[1:1 + 2 * pairs:2].set(donor - moved).at[2:2 + 2 * pairs:2].set(receiver + moved)
    return sizes[jax.random.permutation(jax.random.fold_in(own_key, 2), amount)]


def centred(own_key, dims, scale, reach, shards=(), kind=jnp.bfloat16):
    values = scale * jax.random.normal(own_key, dims, jnp.float32)
    if shards:
        values = values * shard_levels(own_key, dims, shards, -0.22, 0.18)
    return jnp.clip(values, -reach, reach).astype(kind)


def setup_inputs(seed: int = 0) -> dict:
    splits = jax.random.split(jax.random.key(seed), 10)
    return {
        "tokens": centred(splits[0], (TOKENS, D), 1.0, 6.0, ((0, 64),)),
        "norm_gain": jnp.clip(1.0 + 0.15 * jax.random.normal(splits[1], (D,), jnp.float32), 0.25, 1.75),
        "w_query": draw_w_query(jax.random.fold_in(splits[9], 71), 0),
        "w_key": draw_w_key(jax.random.fold_in(splits[9], 71), 0),
        "w_value": centred(splits[4], (D, HEADS * VD), D ** -0.5, 0.125, ((1, 4),)),
        "w_out": centred(splits[5], (HEADS * VD, D), (HEADS * VD) ** -0.5, 0.125, ((0, 4),)),
        "lambdas": draw_lambdas(jax.random.fold_in(splits[9], 71), 0),
        "sub_gain": jnp.clip(jnp.exp(math.log(2.0) - 1.3862944 * jax.random.uniform(splits[7], (HEADS, VD), jnp.float32) ** shard_levels(splits[7], (HEADS, VD), ((0, 4),), -0.2, 0.2)), 0.5, 2.0),
        "lengths": ragged(splits[8], NPROMPTS, TOKENS, MAXLEN, 2).astype(jnp.int32),
    }


lambda_start = 0.8 - 0.6 * math.exp(-3.3)
masked_score = -1e+30

def locate(index, lengths):
    ends = jnp.cumsum(lengths).astype(jnp.int32)
    starts = ends - lengths
    segment = lax.optimization_barrier(jnp.sum((ends[None, :] <= index[:, None]).astype(jnp.int32), axis=1)).astype(jnp.int32)
    hit = jnp.arange(lengths.shape[0], dtype=jnp.int32)[None, :] == segment[:, None]
    begin = lax.optimization_barrier(jnp.sum(jnp.where(hit, starts[None, :], 0), axis=1)).astype(jnp.int32)
    return (segment, index - begin)

def rotate(proj, position):
    half = proj.shape[-1] // 2
    freq = 10000.0 ** (-jnp.arange(half, dtype=jnp.float32) / half)
    angle = position.astype(jnp.float32)[:, None] * freq[None, :]
    cosine = jnp.cos(angle)[:, None, None, :]
    sine = jnp.sin(angle)[:, None, None, :]
    front = proj[..., :half]
    back = proj[..., half:]
    return jnp.concatenate([front * cosine - back * sine, back * cosine + front * sine], axis=-1)

def reference(tokens, norm_gain, w_query, w_key, w_value, w_out, lambdas, sub_gain, lengths):
    xf = tokens.astype(jnp.float32)
    normed = (xf * lax.rsqrt(lax.optimization_barrier(jnp.mean(xf * xf, axis=-1, keepdims=True)) + 1e-06) * norm_gain).astype(jnp.bfloat16)
    index = jnp.arange(TOKENS, dtype=jnp.int32)
    segment, position = locate(index, lengths)
    query = rotate(jnp.dot(normed, w_query, preferred_element_type=jnp.float32).reshape(TOKENS, HEADS, 2, QK), position).astype(jnp.bfloat16)
    keys = rotate(jnp.dot(normed, w_key, preferred_element_type=jnp.float32).reshape(TOKENS, HEADS, 2, QK), position).astype(jnp.bfloat16)
    values = jnp.dot(normed, w_value, preferred_element_type=jnp.float32).astype(jnp.bfloat16)
    lam = jnp.exp(lax.optimization_barrier(jnp.sum(lambdas[0] * lambdas[1], axis=-1))) - jnp.exp(lax.optimization_barrier(jnp.sum(lambdas[2] * lambdas[3], axis=-1))) + lambda_start
    window = MAXLEN + TOK_DEV
    key_pad = jnp.concatenate([jnp.zeros((window, HEADS, 2, QK), jnp.bfloat16), keys], axis=0)
    value_pad = jnp.concatenate([jnp.zeros((window, HEADS, VD), jnp.bfloat16), values.reshape(TOKENS, HEADS, VD)], axis=0)
    seg_pad = jnp.concatenate([jnp.full((window,), -1, jnp.int32), segment], axis=0)
    scale = QK ** (-0.5)

    def block(number):
        begin = (number * TOK_DEV).astype(jnp.int32)
        q_block = lax.dynamic_slice_in_dim(query, begin, TOK_DEV, 0)
        q_seg = lax.dynamic_slice_in_dim(segment, begin, TOK_DEV, 0)
        k_block = lax.dynamic_slice_in_dim(key_pad, begin + TOK_DEV, window, 0)
        v_block = lax.dynamic_slice_in_dim(value_pad, begin + TOK_DEV, window, 0)
        k_seg = lax.dynamic_slice_in_dim(seg_pad, begin + TOK_DEV, window, 0)
        key_index = begin + TOK_DEV - window + jnp.arange(window, dtype=jnp.int32)
        q_index = begin + jnp.arange(TOK_DEV, dtype=jnp.int32)
        allowed = (key_index >= 0)[None, :] & (key_index[None, :] <= q_index[:, None]) & (k_seg[None, :] == q_seg[:, None])
        scores = jnp.einsum('qhmd,khmd->mhqk', q_block.astype(jnp.float32), k_block.astype(jnp.float32), precision=lax.Precision.HIGHEST) * scale
        scores = jnp.where(allowed, scores, masked_score)
        top = lax.optimization_barrier(jnp.max(scores, axis=-1, keepdims=True))
        weights = jnp.where(allowed, jnp.exp(scores - top), 0.0)
        rounded = lax.optimization_barrier(weights.astype(jnp.bfloat16)).astype(jnp.float32)
        attended = jnp.einsum('mhqk,khv->mhqv', rounded, v_block.astype(jnp.float32), precision=lax.Precision.HIGHEST) / lax.optimization_barrier(jnp.sum(weights, axis=-1))[..., None]
        diff = attended[0] - lam[:, None, None] * attended[1]
        normed_heads = diff * lax.rsqrt(lax.optimization_barrier(jnp.mean(diff * diff, axis=-1, keepdims=True)) + 1e-05) * sub_gain[:, None, :] * (1.0 - lambda_start)
        return jnp.transpose(normed_heads, (1, 0, 2)).reshape(TOK_DEV, HEADS * VD).astype(jnp.bfloat16)
    merged = lax.map(block, jnp.arange(TOKENS // TOK_DEV, dtype=jnp.int32)).reshape(TOKENS, HEADS * VD)
    summed = jnp.dot(merged, w_out, preferred_element_type=jnp.float32)
    hidden = (xf + summed).astype(jnp.bfloat16)
    return (hidden, keys.reshape(TOKENS, HEADS * 2 * QK), values)
```

```python
import math

import jax
import jax.numpy as jnp
from jax import lax
from jax.sharding import PartitionSpec as P

QK = 128
VD = 256


lambda_start = 0.8 - 0.6 * math.exp(-3.3)
masked_score = -1e30


def shifted(value, axis, steps):
    count = lax.axis_size(axis)
    first, last = (max(0, -steps), min(count, count - steps))
    return lax.ppermute(value, axis, [(source, source + steps) for source in range(first, last)])


def locate(index, lengths):
    ends = jnp.cumsum(lengths)
    starts = ends - lengths
    segment = jnp.sum((ends[None, :] <= index[:, None]).astype(jnp.int32), axis=1)
    hit = jnp.arange(lengths.shape[0], dtype=jnp.int32)[None, :] == segment[:, None]
    begin = jnp.sum(jnp.where(hit, starts[None, :], 0), axis=1)
    return (segment, index - begin)


def rotate(proj, position):
    half = proj.shape[-1] // 2
    freq = 10000.0 ** (-jnp.arange(half, dtype=jnp.float32) / half)
    angle = position.astype(jnp.float32)[:, None] * freq[None, :]
    cosine = jnp.cos(angle)[:, None, None, :]
    sine = jnp.sin(angle)[:, None, None, :]
    front = proj[..., :half]
    back = proj[..., half:]
    return jnp.concatenate([front * cosine - back * sine, back * cosine + front * sine], axis=-1)


def on_device(tokens, norm_gain, w_query, w_key, w_value, w_out, lambdas, sub_gain, lengths):
    rows = tokens.shape[0]
    heads = w_query.shape[1] // (2 * QK)
    key_cols = heads * 2 * QK
    total = rows * lax.axis_size("req")
    longest = min(8192, total // 2)
    reach = longest // rows
    first = lax.axis_index("req") * rows
    local_index = first + jnp.arange(rows, dtype=jnp.int32)
    seg_query, pos_query = locate(local_index, lengths)
    xf = tokens.astype(jnp.float32)
    normed = (xf * lax.rsqrt(jnp.mean(xf * xf, axis=-1, keepdims=True) + 1e-06) * norm_gain).astype(
        jnp.bfloat16
    )
    query = rotate(
        jnp.dot(normed, w_query, preferred_element_type=jnp.float32).reshape(rows, heads, 2, QK),
        pos_query,
    ).astype(jnp.bfloat16)
    keys = rotate(
        jnp.dot(normed, w_key, preferred_element_type=jnp.float32).reshape(rows, heads, 2, QK),
        pos_query,
    ).astype(jnp.bfloat16)
    values = jnp.dot(normed, w_value, preferred_element_type=jnp.float32).astype(jnp.bfloat16)
    key_flat = keys.reshape(rows, key_cols)
    own = jnp.concatenate([key_flat, values], axis=1)
    lam = (
        jnp.exp(jnp.sum(lambdas[0] * lambdas[1], axis=-1))
        - jnp.exp(jnp.sum(lambdas[2] * lambdas[3], axis=-1))
        + lambda_start
    )
    scale = QK ** (-0.5)

    def absorb(state, shard, anchor):
        key_index = anchor + jnp.arange(rows, dtype=jnp.int32)
        key_seg, unused = locate(key_index, lengths)
        allowed = (
            (key_index >= 0)[None, :]
            & (key_index[None, :] <= local_index[:, None])
            & (key_seg[None, :] == seg_query[:, None])
        )

        def compute(carry):
            top, mass, acc = carry
            shard_keys = shard[:, :key_cols].reshape(rows, heads, 2, QK)
            shard_values = shard[:, key_cols:].reshape(rows, heads, VD)
            scores = (
                jnp.einsum("qhmd,khmd->mhqk", query, shard_keys, preferred_element_type=jnp.float32)
                * scale
            )
            scores = jnp.where(allowed, scores, masked_score)
            new_top = jnp.maximum(top, jnp.max(scores, axis=-1))
            weights = jnp.where(allowed, jnp.exp(scores - new_top[..., None]), 0.0)
            fade = jnp.exp(top - new_top)
            mass = mass * fade + jnp.sum(weights, axis=-1)
            acc = acc * fade[..., None] + jnp.einsum(
                "mhqk,khv->mhqv",
                weights.astype(jnp.bfloat16),
                shard_values,
                preferred_element_type=jnp.float32,
            )
            return (new_top, mass, acc)

        def keep(carry):
            return carry

        return lax.cond(jnp.any(allowed), compute, keep, state)

    start = (
        jnp.full((2, heads, rows), masked_score, jnp.float32),
        jnp.zeros((2, heads, rows), jnp.float32),
        jnp.zeros((2, heads, rows, VD), jnp.float32),
    )
    arriving = shifted(own, "req", 1)
    state = absorb(start, own, first)

    def turn(step, carry):
        current, moving = carry
        following = shifted(moving, "req", 1)
        return (absorb(current, moving, first - (step + 1) * rows), following)

    state, moving = lax.fori_loop(0, reach - 1, turn, (state, arriving))
    state = absorb(state, moving, first - reach * rows)
    top, mass, acc = state
    attended = acc / mass[..., None]
    diff = attended[0] - lam[:, None, None] * attended[1]
    normed_heads = (
        diff
        * lax.rsqrt(jnp.mean(diff * diff, axis=-1, keepdims=True) + 1e-05)
        * sub_gain[:, None, :]
        * (1.0 - lambda_start)
    )
    merged = jnp.transpose(normed_heads, (1, 0, 2)).reshape(rows, heads * VD).astype(jnp.bfloat16)
    summed = lax.psum(
        jnp.dot(merged, w_out, preferred_element_type=jnp.float32).astype(jnp.bfloat16), "tp"
    ).astype(jnp.float32)
    hidden = (xf + summed).astype(jnp.bfloat16)
    return (hidden, key_flat, values)


def solution(mesh):
    in_specs = (
        P("req", None),
        P(),
        P(None, "tp"),
        P(None, "tp"),
        P(None, "tp"),
        P("tp", None),
        P(None, "tp", None),
        P("tp", None),
        P(),
    )
    out_specs = (P("req", None), P("req", "tp"), P("req", "tp"))
    return jax.shard_map(
        on_device, mesh=mesh, in_specs=in_specs, out_specs=out_specs, check_vma=False
    )
```

```python
import math

import jax
import jax.numpy as jnp
from jax import lax
from jax.sharding import Mesh
from jax.sharding import PartitionSpec as P

QK = 128
VD = 256
MAXLEN = 8192


lambda_start = 0.8 - 0.6 * math.exp(-3.3)
masked_score = -1e30


def locate(index, lengths):
    ends = jnp.cumsum(lengths)
    starts = ends - lengths
    segment = jnp.sum((ends[None, :] <= index[:, None]).astype(jnp.int32), axis=1)
    hit = jnp.arange(lengths.shape[0], dtype=jnp.int32)[None, :] == segment[:, None]
    begin = jnp.sum(jnp.where(hit, starts[None, :], 0), axis=1)
    return (segment, index - begin)


def rotate(proj, position):
    half = proj.shape[-1] // 2
    freq = 10000.0 ** (-jnp.arange(half, dtype=jnp.float32) / half)
    angle = position.astype(jnp.float32)[:, None] * freq[None, :]
    cosine = jnp.cos(angle)[:, None, None, :]
    sine = jnp.sin(angle)[:, None, None, :]
    front = proj[..., :half]
    back = proj[..., half:]
    return jnp.concatenate([front * cosine - back * sine, back * cosine + front * sine], axis=-1)


def swap_cores(value):
    return lax.ppermute(value, "core", [(0, 1), (1, 0)])


def on_device(tokens, norm_gain, w_query, w_key, w_value, w_out, lambdas, sub_gain, lengths):
    rows = tokens.shape[0]
    heads = w_query.shape[1] // (2 * QK)
    key_cols = heads * 2 * QK
    chips = lax.axis_size("chip")
    total = rows * 2 * chips
    core = lax.axis_index("core")
    chip = lax.axis_index("chip")
    first = (chip * 2 + core) * rows
    local_index = first + jnp.arange(rows, dtype=jnp.int32)
    unused, pos_own = locate(local_index, lengths)
    xf = tokens.astype(jnp.float32)
    normed = (xf * lax.rsqrt(jnp.mean(xf * xf, axis=-1, keepdims=True) + 1e-06) * norm_gain).astype(
        jnp.bfloat16
    )
    query = rotate(
        jnp.dot(normed, w_query, preferred_element_type=jnp.float32).reshape(rows, heads, 2, QK),
        pos_own,
    ).astype(jnp.bfloat16)
    keys = rotate(
        jnp.dot(normed, w_key, preferred_element_type=jnp.float32).reshape(rows, heads, 2, QK),
        pos_own,
    ).astype(jnp.bfloat16)
    values = jnp.dot(normed, w_value, preferred_element_type=jnp.float32).astype(jnp.bfloat16)
    key_flat = keys.reshape(rows, key_cols)
    lam = (
        jnp.exp(jnp.sum(lambdas[0] * lambdas[1], axis=-1))
        - jnp.exp(jnp.sum(lambdas[2] * lambdas[3], axis=-1))
        + lambda_start
    )
    scale = QK ** (-0.5)

    def head_part(h):
        q_h = lax.dynamic_index_in_dim(query, h, axis=1, keepdims=False).reshape(rows, 2 * QK)
        k_h = lax.dynamic_index_in_dim(keys, h, axis=1, keepdims=False).reshape(rows, 2 * QK)
        v_h = lax.dynamic_index_in_dim(values.reshape(rows, heads, VD), h, axis=1, keepdims=False)
        return jnp.concatenate([q_h, k_h, v_h], axis=1)

    mine = head_part(core)
    theirs = swap_cores(head_part(1 - core))
    pair = jnp.where(core == 0, jnp.concatenate([mine, theirs], axis=0), jnp.concatenate([theirs, mine], axis=0))
    span = 2 * rows
    q_pair = pair[:, : 2 * QK].reshape(span, 2, QK)
    kv_pair = pair[:, 2 * QK :]
    gathered = lax.all_gather(kv_pair, "chip", axis=0, tiled=True)

    window = min(MAXLEN + span, total)
    base = chip * span
    start = jnp.clip(base + span - window, 0, total - window)
    q_index = base + jnp.arange(span, dtype=jnp.int32)
    key_index = start + jnp.arange(window, dtype=jnp.int32)
    q_seg, unused = locate(q_index, lengths)
    k_seg, unused = locate(key_index, lengths)
    allowed = (key_index[None, :] <= q_index[:, None]) & (k_seg[None, :] == q_seg[:, None])
    kv_win = lax.dynamic_slice_in_dim(gathered, start, window, axis=0)
    v_win = kv_win[:, 2 * QK :]

    def attend(m):
        k_m = kv_win[:, m * QK : (m + 1) * QK]
        scores = jnp.einsum("qd,kd->qk", q_pair[:, m, :], k_m, preferred_element_type=jnp.float32) * scale
        scores = jnp.where(allowed, scores, masked_score)
        top = jnp.max(scores, axis=-1, keepdims=True)
        weights = jnp.where(allowed, jnp.exp(scores - top), 0.0)
        mass = jnp.sum(weights, axis=-1, keepdims=True)
        acc = jnp.dot(weights.astype(jnp.bfloat16), v_win, preferred_element_type=jnp.float32)
        return acc / mass

    lam_h = lax.dynamic_index_in_dim(lam, core, keepdims=False)
    gain_h = lax.dynamic_index_in_dim(sub_gain, core, axis=0, keepdims=False)
    diff = attend(0) - lam_h * attend(1)
    head_out = (
        diff * lax.rsqrt(jnp.mean(diff * diff, axis=-1, keepdims=True) + 1e-05) * gain_h * (1.0 - lambda_start)
    ).astype(jnp.bfloat16)
    own_rows = lax.dynamic_slice_in_dim(head_out, core * rows, rows, axis=0)
    other_rows = swap_cores(lax.dynamic_slice_in_dim(head_out, (1 - core) * rows, rows, axis=0))
    merged = jnp.where(
        core == 0,
        jnp.concatenate([own_rows, other_rows], axis=1),
        jnp.concatenate([other_rows, own_rows], axis=1),
    )
    summed = lax.psum(
        jnp.dot(merged, w_out, preferred_element_type=jnp.float32).astype(jnp.bfloat16), "tp"
    ).astype(jnp.float32)
    hidden = (xf + summed).astype(jnp.bfloat16)
    return (hidden, key_flat, values)


def solution(mesh):
    req, tp = mesh.shape["req"], mesh.shape["tp"]
    paired = Mesh(mesh.devices.reshape(req // 2, 2, tp), ("chip", "core", "tp"))
    rows = ("chip", "core")
    in_specs = (
        P(rows, None),
        P(),
        P(None, "tp"),
        P(None, "tp"),
        P(None, "tp"),
        P("tp", None),
        P(None, "tp", None),
        P("tp", None),
        P(),
    )
    out_specs = (P(rows, None), P(rows, "tp"), P(rows, "tp"))
    return jax.shard_map(
        on_device, mesh=paired, in_specs=in_specs, out_specs=out_specs, check_vma=False
    )
```

```python
import math

import jax
import jax.numpy as jnp
from jax import lax
from jax.sharding import Mesh
from jax.sharding import PartitionSpec as P

QK = 128
VD = 256
MAXLEN = 8192


lambda_start = 0.8 - 0.6 * math.exp(-3.3)
masked_score = -1e30


def locate(index, lengths):
    ends = jnp.cumsum(lengths)
    starts = ends - lengths
    segment = jnp.sum((ends[None, :] <= index[:, None]).astype(jnp.int32), axis=1)
    hit = jnp.arange(lengths.shape[0], dtype=jnp.int32)[None, :] == segment[:, None]
    begin = jnp.sum(jnp.where(hit, starts[None, :], 0), axis=1)
    return (segment, index - begin)


def rotate(proj, position):
    half = proj.shape[-1] // 2
    freq = 10000.0 ** (-jnp.arange(half, dtype=jnp.float32) / half)
    angle = position.astype(jnp.float32)[:, None] * freq[None, :]
    cosine = jnp.cos(angle)[:, None, None, :]
    sine = jnp.sin(angle)[:, None, None, :]
    front = proj[..., :half]
    back = proj[..., half:]
    return jnp.concatenate([front * cosine - back * sine, back * cosine + front * sine], axis=-1)


def swap_cores(value):
    return lax.ppermute(value, "core", [(0, 1), (1, 0)])


def on_device(tokens, norm_gain, w_query, w_key, w_value, w_out, lambdas, sub_gain, lengths):
    rows = tokens.shape[0]
    heads = w_query.shape[1] // (2 * QK)
    key_cols = heads * 2 * QK
    chips = lax.axis_size("chip")
    total = rows * 2 * chips
    core = lax.axis_index("core")
    chip = lax.axis_index("chip")
    first = (chip * 2 + core) * rows
    local_index = first + jnp.arange(rows, dtype=jnp.int32)
    unused, pos_own = locate(local_index, lengths)
    xf = tokens.astype(jnp.float32)
    normed = (xf * lax.rsqrt(jnp.mean(xf * xf, axis=-1, keepdims=True) + 1e-06) * norm_gain).astype(
        jnp.bfloat16
    )
    query = rotate(
        jnp.dot(normed, w_query, preferred_element_type=jnp.float32).reshape(rows, heads, 2, QK),
        pos_own,
    ).astype(jnp.bfloat16)
    keys = rotate(
        jnp.dot(normed, w_key, preferred_element_type=jnp.float32).reshape(rows, heads, 2, QK),
        pos_own,
    ).astype(jnp.bfloat16)
    values = jnp.dot(normed, w_value, preferred_element_type=jnp.float32).astype(jnp.bfloat16)
    key_flat = keys.reshape(rows, key_cols)
    lam = (
        jnp.exp(jnp.sum(lambdas[0] * lambdas[1], axis=-1))
        - jnp.exp(jnp.sum(lambdas[2] * lambdas[3], axis=-1))
        + lambda_start
    )
    scale = QK ** (-0.5)

    def head_part(h):
        q_h = lax.dynamic_index_in_dim(query, h, axis=1, keepdims=False).reshape(rows, 2 * QK)
        k_h = lax.dynamic_index_in_dim(keys, h, axis=1, keepdims=False).reshape(rows, 2 * QK)
        v_h = lax.dynamic_index_in_dim(values.reshape(rows, heads, VD), h, axis=1, keepdims=False)
        return jnp.concatenate([q_h, k_h, v_h], axis=1)

    mine = head_part(core)
    theirs = swap_cores(head_part(1 - core))
    pair = jnp.where(core == 0, jnp.concatenate([mine, theirs], axis=0), jnp.concatenate([theirs, mine], axis=0))
    span = 2 * rows
    q_pair = pair[:, : 2 * QK].reshape(span, 2, QK)
    own_gathered = lax.all_gather(mine[:, 2 * QK :], "chip", axis=0, tiled=True)
    other_gathered = lax.all_gather(theirs[:, 2 * QK :], "chip", axis=0, tiled=True)

    reach = min(MAXLEN // span + 1, chips)
    first_chip = jnp.clip(chip + 1 - reach, 0, chips - reach)
    base = chip * span
    q_index = base + jnp.arange(span, dtype=jnp.int32)
    q_seg, unused = locate(q_index, lengths)
    slot = jnp.arange(reach * rows, dtype=jnp.int32)

    def part(gathered, half):
        key_index = (first_chip + slot // rows) * span + half * rows + slot % rows
        k_seg, unused = locate(key_index, lengths)
        allowed = (key_index[None, :] <= q_index[:, None]) & (k_seg[None, :] == q_seg[:, None])
        kv_win = lax.dynamic_slice_in_dim(gathered, first_chip * rows, reach * rows, axis=0)
        v_win = kv_win[:, 2 * QK :]
        stats = []
        for m in range(2):
            k_m = kv_win[:, m * QK : (m + 1) * QK]
            scores = jnp.einsum("qd,kd->qk", q_pair[:, m, :], k_m, preferred_element_type=jnp.float32) * scale
            scores = jnp.where(allowed, scores, masked_score)
            top = jnp.max(scores, axis=-1, keepdims=True)
            weights = jnp.where(allowed, jnp.exp(scores - top), 0.0)
            mass = jnp.sum(weights, axis=-1, keepdims=True)
            acc = jnp.dot(weights.astype(jnp.bfloat16), v_win, preferred_element_type=jnp.float32)
            stats.append((top, mass, acc))
        return stats

    own_stats = part(own_gathered, core)
    own_stats, other_gathered = lax.optimization_barrier((own_stats, other_gathered))
    other_stats = part(other_gathered, 1 - core)

    def attend(m):
        top_a, mass_a, acc_a = own_stats[m]
        top_b, mass_b, acc_b = other_stats[m]
        top = jnp.maximum(top_a, top_b)
        fade_a = jnp.exp(top_a - top)
        fade_b = jnp.exp(top_b - top)
        return (acc_a * fade_a + acc_b * fade_b) / (mass_a * fade_a + mass_b * fade_b)

    lam_h = lax.dynamic_index_in_dim(lam, core, keepdims=False)
    gain_h = lax.dynamic_index_in_dim(sub_gain, core, axis=0, keepdims=False)
    diff = attend(0) - lam_h * attend(1)
    head_out = (
        diff * lax.rsqrt(jnp.mean(diff * diff, axis=-1, keepdims=True) + 1e-05) * gain_h * (1.0 - lambda_start)
    ).astype(jnp.bfloat16)
    own_rows = lax.dynamic_slice_in_dim(head_out, core * rows, rows, axis=0)
    other_rows = swap_cores(lax.dynamic_slice_in_dim(head_out, (1 - core) * rows, rows, axis=0))
    merged = jnp.where(
        core == 0,
        jnp.concatenate([own_rows, other_rows], axis=1),
        jnp.concatenate([other_rows, own_rows], axis=1),
    )
    summed = lax.psum(
        jnp.dot(merged, w_out, preferred_element_type=jnp.float32).astype(jnp.bfloat16), "tp"
    ).astype(jnp.float32)
    hidden = (xf + summed).astype(jnp.bfloat16)
    return (hidden, key_flat, values)


def solution(mesh):
    req, tp = mesh.shape["req"], mesh.shape["tp"]
    paired = Mesh(mesh.devices.reshape(req // 2, 2, tp), ("chip", "core", "tp"))
    rows = ("chip", "core")
    in_specs = (
        P(rows, None),
        P(),
        P(None, "tp"),
        P(None, "tp"),
        P(None, "tp"),
        P("tp", None),
        P(None, "tp", None),
        P("tp", None),
        P(),
    )
    out_specs = (P(rows, None), P(rows, "tp"), P(rows, "tp"))
    return jax.shard_map(
        on_device, mesh=paired, in_specs=in_specs, out_specs=out_specs, check_vma=False
    )
```

```python
import math

import jax
import jax.numpy as jnp
from jax import lax
from jax.sharding import Mesh
from jax.sharding import PartitionSpec as P

QK = 128
VD = 256
MAXLEN = 8192


lambda_start = 0.8 - 0.6 * math.exp(-3.3)
masked_score = -1e30


def locate(index, lengths):
    ends = jnp.cumsum(lengths)
    starts = ends - lengths
    segment = jnp.sum((ends[None, :] <= index[:, None]).astype(jnp.int32), axis=1)
    hit = jnp.arange(lengths.shape[0], dtype=jnp.int32)[None, :] == segment[:, None]
    begin = jnp.sum(jnp.where(hit, starts[None, :], 0), axis=1)
    return (segment, index - begin)


def rotate(proj, position):
    half = proj.shape[-1] // 2
    freq = 10000.0 ** (-jnp.arange(half, dtype=jnp.float32) / half)
    angle = position.astype(jnp.float32)[:, None] * freq[None, :]
    cosine = jnp.cos(angle)[:, None, None, :]
    sine = jnp.sin(angle)[:, None, None, :]
    front = proj[..., :half]
    back = proj[..., half:]
    return jnp.concatenate([front * cosine - back * sine, back * cosine + front * sine], axis=-1)


def swap_cores(value):
    return lax.ppermute(value, "core", [(0, 1), (1, 0)])


def on_device(tokens, norm_gain, w_query, w_key, w_value, w_out, lambdas, sub_gain, lengths):
    rows = tokens.shape[0]
    heads = w_query.shape[1] // (2 * QK)
    key_cols = heads * 2 * QK
    chips = lax.axis_size("chip")
    total = rows * 2 * chips
    core = lax.axis_index("core")
    chip = lax.axis_index("chip")
    first = (chip * 2 + core) * rows
    local_index = first + jnp.arange(rows, dtype=jnp.int32)
    unused, pos_own = locate(local_index, lengths)
    xf = tokens.astype(jnp.float32)
    normed = (xf * lax.rsqrt(jnp.mean(xf * xf, axis=-1, keepdims=True) + 1e-06) * norm_gain).astype(
        jnp.bfloat16
    )
    keys = rotate(
        jnp.dot(normed, w_key, preferred_element_type=jnp.float32).reshape(rows, heads, 2, QK),
        pos_own,
    ).astype(jnp.bfloat16)
    values = jnp.dot(normed, w_value, preferred_element_type=jnp.float32).astype(jnp.bfloat16)
    key_flat = keys.reshape(rows, key_cols)
    lam = (
        jnp.exp(jnp.sum(lambdas[0] * lambdas[1], axis=-1))
        - jnp.exp(jnp.sum(lambdas[2] * lambdas[3], axis=-1))
        + lambda_start
    )
    scale = QK ** (-0.5)

    def head_kv(h):
        k_h = lax.dynamic_index_in_dim(keys, h, axis=1, keepdims=False).reshape(rows, 2 * QK)
        v_h = lax.dynamic_index_in_dim(values.reshape(rows, heads, VD), h, axis=1, keepdims=False)
        return jnp.concatenate([k_h, v_h], axis=1)

    def in_order(mine, theirs):
        return jnp.where(core == 0, jnp.concatenate([mine, theirs], axis=0), jnp.concatenate([theirs, mine], axis=0))

    span = 2 * rows
    kv_pair = in_order(head_kv(core), swap_cores(head_kv(1 - core)))
    gathered = lax.all_gather(kv_pair, "chip", axis=0, tiled=True)
    query = rotate(
        jnp.dot(normed, w_query, preferred_element_type=jnp.float32).reshape(rows, heads, 2, QK),
        pos_own,
    ).astype(jnp.bfloat16)
    q_pair = in_order(
        lax.dynamic_index_in_dim(query, core, axis=1, keepdims=False),
        swap_cores(lax.dynamic_index_in_dim(query, 1 - core, axis=1, keepdims=False)),
    )

    window = min(MAXLEN + span, total)
    base = chip * span
    start = jnp.clip(base + span - window, 0, total - window)
    q_index = base + jnp.arange(span, dtype=jnp.int32)
    q_seg, unused = locate(q_index, lengths)
    pieces = 2
    piece = window // pieces

    def part(p):
        key_index = start + p * piece + jnp.arange(piece, dtype=jnp.int32)
        k_seg, unused = locate(key_index, lengths)
        allowed = (key_index[None, :] <= q_index[:, None]) & (k_seg[None, :] == q_seg[:, None])
        kv_win = lax.dynamic_slice_in_dim(gathered, start + p * piece, piece, axis=0)
        v_win = kv_win[:, 2 * QK :]
        stats = []
        for m in range(2):
            k_m = kv_win[:, m * QK : (m + 1) * QK]
            scores = jnp.einsum("qd,kd->qk", q_pair[:, m, :], k_m, preferred_element_type=jnp.float32) * scale
            scores = jnp.where(allowed, scores, masked_score)
            top = jnp.max(scores, axis=-1, keepdims=True)
            weights = jnp.where(allowed, jnp.exp(scores - top), 0.0)
            mass = jnp.sum(weights, axis=-1, keepdims=True)
            acc = jnp.dot(weights.astype(jnp.bfloat16), v_win, preferred_element_type=jnp.float32)
            stats.append((top, mass, acc))
        return stats

    all_stats = [part(p) for p in range(pieces)]

    def attend(m):
        tops = [stats[m][0] for stats in all_stats]
        top = tops[0]
        for other in tops[1:]:
            top = jnp.maximum(top, other)
        acc = 0.0
        mass = 0.0
        for stats in all_stats:
            fade = jnp.exp(stats[m][0] - top)
            mass = mass + stats[m][1] * fade
            acc = acc + stats[m][2] * fade
        return acc / mass

    lam_h = lax.dynamic_index_in_dim(lam, core, keepdims=False)
    gain_h = lax.dynamic_index_in_dim(sub_gain, core, axis=0, keepdims=False)
    diff = attend(0) - lam_h * attend(1)
    head_out = (
        diff * lax.rsqrt(jnp.mean(diff * diff, axis=-1, keepdims=True) + 1e-05) * gain_h * (1.0 - lambda_start)
    ).astype(jnp.bfloat16)
    own_rows = lax.dynamic_slice_in_dim(head_out, core * rows, rows, axis=0)
    other_rows = swap_cores(lax.dynamic_slice_in_dim(head_out, (1 - core) * rows, rows, axis=0))
    merged = jnp.where(
        core == 0,
        jnp.concatenate([own_rows, other_rows], axis=1),
        jnp.concatenate([other_rows, own_rows], axis=1),
    )
    summed = lax.psum(
        jnp.dot(merged, w_out, preferred_element_type=jnp.float32).astype(jnp.bfloat16), "tp"
    ).astype(jnp.float32)
    hidden = (xf + summed).astype(jnp.bfloat16)
    return (hidden, key_flat, values)


def solution(mesh):
    req, tp = mesh.shape["req"], mesh.shape["tp"]
    paired = Mesh(mesh.devices.reshape(req // 2, 2, tp), ("chip", "core", "tp"))
    rows = ("chip", "core")
    in_specs = (
        P(rows, None),
        P(),
        P(None, "tp"),
        P(None, "tp"),
        P(None, "tp"),
        P("tp", None),
        P(None, "tp", None),
        P("tp", None),
        P(),
    )
    out_specs = (P(rows, None), P(rows, "tp"), P(rows, "tp"))
    return jax.shard_map(
        on_device, mesh=paired, in_specs=in_specs, out_specs=out_specs, check_vma=False
    )
```

```python
import math

import jax
import jax.numpy as jnp
from jax import lax
from jax.sharding import Mesh
from jax.sharding import PartitionSpec as P

QK = 128
VD = 256
MAXLEN = 8192


lambda_start = 0.8 - 0.6 * math.exp(-3.3)
masked_score = -1e30


def locate(index, lengths):
    ends = jnp.cumsum(lengths)
    starts = ends - lengths
    segment = jnp.sum((ends[None, :] <= index[:, None]).astype(jnp.int32), axis=1)
    hit = jnp.arange(lengths.shape[0], dtype=jnp.int32)[None, :] == segment[:, None]
    begin = jnp.sum(jnp.where(hit, starts[None, :], 0), axis=1)
    return (segment, index - begin)


def rotate(proj, position):
    half = proj.shape[-1] // 2
    freq = 10000.0 ** (-jnp.arange(half, dtype=jnp.float32) / half)
    angle = position.astype(jnp.float32)[:, None] * freq[None, :]
    cosine = jnp.cos(angle)[:, None, None, :]
    sine = jnp.sin(angle)[:, None, None, :]
    front = proj[..., :half]
    back = proj[..., half:]
    return jnp.concatenate([front * cosine - back * sine, back * cosine + front * sine], axis=-1)


def swap_cores(value):
    return lax.ppermute(value, "core", [(0, 1), (1, 0)])


def on_device(tokens, norm_gain, w_query, w_key, w_value, w_out, lambdas, sub_gain, lengths):
    rows = tokens.shape[0]
    heads = w_query.shape[1] // (2 * QK)
    key_cols = heads * 2 * QK
    ys, zs, xs = lax.axis_size("y"), lax.axis_size("z"), lax.axis_size("x")
    chips = ys * zs * xs
    total = rows * 2 * chips
    core = lax.axis_index("core")
    chip = (lax.axis_index("y") * zs + lax.axis_index("z")) * xs + lax.axis_index("x")
    first = (chip * 2 + core) * rows
    local_index = first + jnp.arange(rows, dtype=jnp.int32)
    unused, pos_own = locate(local_index, lengths)
    xf = tokens.astype(jnp.float32)
    normed = (xf * lax.rsqrt(jnp.mean(xf * xf, axis=-1, keepdims=True) + 1e-06) * norm_gain).astype(
        jnp.bfloat16
    )
    keys = rotate(
        jnp.dot(normed, w_key, preferred_element_type=jnp.float32).reshape(rows, heads, 2, QK),
        pos_own,
    ).astype(jnp.bfloat16)
    values = jnp.dot(normed, w_value, preferred_element_type=jnp.float32).astype(jnp.bfloat16)
    key_flat = keys.reshape(rows, key_cols)
    lam = (
        jnp.exp(jnp.sum(lambdas[0] * lambdas[1], axis=-1))
        - jnp.exp(jnp.sum(lambdas[2] * lambdas[3], axis=-1))
        + lambda_start
    )
    scale = QK ** (-0.5)

    def head_kv(h):
        k_h = lax.dynamic_index_in_dim(keys, h, axis=1, keepdims=False).reshape(rows, 2 * QK)
        v_h = lax.dynamic_index_in_dim(values.reshape(rows, heads, VD), h, axis=1, keepdims=False)
        return jnp.concatenate([k_h, v_h], axis=1)

    def in_order(mine, theirs):
        return jnp.where(core == 0, jnp.concatenate([mine, theirs], axis=0), jnp.concatenate([theirs, mine], axis=0))

    span = 2 * rows
    kv_pair = in_order(head_kv(core), swap_cores(head_kv(1 - core)))
    z = lax.axis_index("z")
    kv_z = lax.ppermute(kv_pair, "z", [(0, 1), (1, 0)])
    kv_quad = jnp.where(z == 0, jnp.concatenate([kv_pair, kv_z], axis=0), jnp.concatenate([kv_z, kv_pair], axis=0))
    gathered = lax.all_gather(kv_quad, ("y", "x"), axis=0, tiled=True)
    query = rotate(
        jnp.dot(normed, w_query, preferred_element_type=jnp.float32).reshape(rows, heads, 2, QK),
        pos_own,
    ).astype(jnp.bfloat16)
    q_pair = in_order(
        lax.dynamic_index_in_dim(query, core, axis=1, keepdims=False),
        swap_cores(lax.dynamic_index_in_dim(query, 1 - core, axis=1, keepdims=False)),
    )

    reach = min(MAXLEN // span + 1, chips)
    window = reach * span
    base = chip * span
    first_chip = jnp.clip(chip + 1 - reach, 0, chips - reach)
    start = first_chip * span
    blocks = []
    for i in range(reach):
        c = first_chip + i
        slot = ((c // (zs * xs)) * xs + c % xs) * zs + (c // xs) % zs
        blocks.append(lax.dynamic_slice_in_dim(gathered, slot * span, span, axis=0))
    kv_window = jnp.concatenate(blocks, axis=0)
    q_index = base + jnp.arange(span, dtype=jnp.int32)
    q_seg, unused = locate(q_index, lengths)
    pieces = 2
    piece = window // pieces

    def part(p):
        key_index = start + p * piece + jnp.arange(piece, dtype=jnp.int32)
        k_seg, unused = locate(key_index, lengths)
        allowed = (key_index[None, :] <= q_index[:, None]) & (k_seg[None, :] == q_seg[:, None])
        kv_win = kv_window[p * piece : (p + 1) * piece]
        v_win = kv_win[:, 2 * QK :]
        stats = []
        for m in range(2):
            k_m = kv_win[:, m * QK : (m + 1) * QK]
            scores = jnp.einsum("qd,kd->qk", q_pair[:, m, :], k_m, preferred_element_type=jnp.float32) * scale
            scores = jnp.where(allowed, scores, masked_score)
            top = jnp.max(scores, axis=-1, keepdims=True)
            weights = jnp.where(allowed, jnp.exp(scores - top), 0.0)
            mass = jnp.sum(weights, axis=-1, keepdims=True)
            acc = jnp.dot(weights.astype(jnp.bfloat16), v_win, preferred_element_type=jnp.float32)
            stats.append((top, mass, acc))
        return stats

    all_stats = [part(p) for p in range(pieces)]

    def attend(m):
        tops = [stats[m][0] for stats in all_stats]
        top = tops[0]
        for other in tops[1:]:
            top = jnp.maximum(top, other)
        acc = 0.0
        mass = 0.0
        for stats in all_stats:
            fade = jnp.exp(stats[m][0] - top)
            mass = mass + stats[m][1] * fade
            acc = acc + stats[m][2] * fade
        return acc / mass

    lam_h = lax.dynamic_index_in_dim(lam, core, keepdims=False)
    gain_h = lax.dynamic_index_in_dim(sub_gain, core, axis=0, keepdims=False)
    diff = attend(0) - lam_h * attend(1)
    head_out = (
        diff * lax.rsqrt(jnp.mean(diff * diff, axis=-1, keepdims=True) + 1e-05) * gain_h * (1.0 - lambda_start)
    ).astype(jnp.bfloat16)
    own_rows = lax.dynamic_slice_in_dim(head_out, core * rows, rows, axis=0)
    other_rows = swap_cores(lax.dynamic_slice_in_dim(head_out, (1 - core) * rows, rows, axis=0))
    merged = jnp.where(
        core == 0,
        jnp.concatenate([own_rows, other_rows], axis=1),
        jnp.concatenate([other_rows, own_rows], axis=1),
    )
    summed = lax.psum(
        jnp.dot(merged, w_out, preferred_element_type=jnp.float32).astype(jnp.bfloat16), "tp"
    ).astype(jnp.float32)
    hidden = (xf + summed).astype(jnp.bfloat16)
    return (hidden, key_flat, values)


def solution(mesh):
    req, tp = mesh.shape["req"], mesh.shape["tp"]
    paired = Mesh(mesh.devices.reshape(req // 16, 2, 4, 2, tp), ("y", "z", "x", "core", "tp"))
    rows = ("y", "z", "x", "core")
    in_specs = (
        P(rows, None),
        P(),
        P(None, "tp"),
        P(None, "tp"),
        P(None, "tp"),
        P("tp", None),
        P(None, "tp", None),
        P("tp", None),
        P(),
    )
    out_specs = (P(rows, None), P(rows, "tp"), P(rows, "tp"))
    return jax.shard_map(
        on_device, mesh=paired, in_specs=in_specs, out_specs=out_specs, check_vma=False
    )
```

```python
import math

import jax
import jax.numpy as jnp
from jax import lax
from jax.sharding import Mesh
from jax.sharding import PartitionSpec as P

QK = 128
VD = 256
MAXLEN = 8192


lambda_start = 0.8 - 0.6 * math.exp(-3.3)
masked_score = -1e30


def locate(index, lengths):
    ends = jnp.cumsum(lengths)
    starts = ends - lengths
    segment = jnp.sum((ends[None, :] <= index[:, None]).astype(jnp.int32), axis=1)
    hit = jnp.arange(lengths.shape[0], dtype=jnp.int32)[None, :] == segment[:, None]
    begin = jnp.sum(jnp.where(hit, starts[None, :], 0), axis=1)
    return (segment, index - begin)


def rotate(proj, position):
    half = proj.shape[-1] // 2
    freq = 10000.0 ** (-jnp.arange(half, dtype=jnp.float32) / half)
    angle = position.astype(jnp.float32)[:, None] * freq[None, :]
    cosine = jnp.cos(angle)[:, None, None, :]
    sine = jnp.sin(angle)[:, None, None, :]
    front = proj[..., :half]
    back = proj[..., half:]
    return jnp.concatenate([front * cosine - back * sine, back * cosine + front * sine], axis=-1)


def swap_cores(value):
    return lax.ppermute(value, "core", [(0, 1), (1, 0)])


def on_device(tokens, norm_gain, w_query, w_key, w_value, w_out, lambdas, sub_gain, lengths):
    rows = tokens.shape[0]
    heads = w_query.shape[1] // (2 * QK)
    key_cols = heads * 2 * QK
    ys, zs, xs = lax.axis_size("y"), lax.axis_size("z"), lax.axis_size("x")
    chips = ys * zs * xs
    total = rows * 2 * chips
    core = lax.axis_index("core")
    chip = (lax.axis_index("y") * zs + lax.axis_index("z")) * xs + lax.axis_index("x")
    first = (chip * 2 + core) * rows
    local_index = first + jnp.arange(rows, dtype=jnp.int32)
    unused, pos_own = locate(local_index, lengths)
    xf = tokens.astype(jnp.float32)
    normed = (xf * lax.rsqrt(jnp.mean(xf * xf, axis=-1, keepdims=True) + 1e-06) * norm_gain).astype(
        jnp.bfloat16
    )
    keys = rotate(
        jnp.dot(normed, w_key, preferred_element_type=jnp.float32).reshape(rows, heads, 2, QK),
        pos_own,
    ).astype(jnp.bfloat16)
    values = jnp.dot(normed, w_value, preferred_element_type=jnp.float32).astype(jnp.bfloat16)
    key_flat = keys.reshape(rows, key_cols)
    lam = (
        jnp.exp(jnp.sum(lambdas[0] * lambdas[1], axis=-1))
        - jnp.exp(jnp.sum(lambdas[2] * lambdas[3], axis=-1))
        + lambda_start
    )
    scale = QK ** (-0.5)

    def head_kv(h):
        k_h = lax.dynamic_index_in_dim(keys, h, axis=1, keepdims=False).reshape(rows, 2 * QK)
        v_h = lax.dynamic_index_in_dim(values.reshape(rows, heads, VD), h, axis=1, keepdims=False)
        return jnp.concatenate([k_h, v_h], axis=1)

    def in_order(mine, theirs):
        return jnp.where(core == 0, jnp.concatenate([mine, theirs], axis=0), jnp.concatenate([theirs, mine], axis=0))

    span = 2 * rows
    kv_pair = in_order(head_kv(core), swap_cores(head_kv(1 - core)))
    z = lax.axis_index("z")
    kv_z = lax.ppermute(kv_pair, "z", [(0, 1), (1, 0)])
    kv_quad = jnp.where(z == 0, jnp.concatenate([kv_pair, kv_z], axis=0), jnp.concatenate([kv_z, kv_pair], axis=0))
    gathered = lax.all_gather(kv_quad, ("y", "x"), axis=0, tiled=True)
    query = rotate(
        jnp.dot(normed, w_query, preferred_element_type=jnp.float32).reshape(rows, heads, 2, QK),
        pos_own,
    ).astype(jnp.bfloat16)
    q_pair = in_order(
        lax.dynamic_index_in_dim(query, core, axis=1, keepdims=False),
        swap_cores(lax.dynamic_index_in_dim(query, 1 - core, axis=1, keepdims=False)),
    )

    reach = min(MAXLEN // span + 1, chips)
    window = reach * span
    base = chip * span
    first_chip = jnp.clip(chip + 1 - reach, 0, chips - reach)
    start = first_chip * span
    c = first_chip + jnp.arange(reach, dtype=jnp.int32)
    slot = ((c // (zs * xs)) * xs + c % xs) * zs + (c // xs) % zs
    kv_window = jnp.take(gathered.reshape(chips, span, -1), slot, axis=0, mode="clip").reshape(window, -1)
    q_index = base + jnp.arange(span, dtype=jnp.int32)
    q_seg, unused = locate(q_index, lengths)
    pieces = 2
    piece = window // pieces

    def part(p):
        key_index = start + p * piece + jnp.arange(piece, dtype=jnp.int32)
        k_seg, unused = locate(key_index, lengths)
        allowed = (key_index[None, :] <= q_index[:, None]) & (k_seg[None, :] == q_seg[:, None])
        kv_win = kv_window[p * piece : (p + 1) * piece]
        v_win = kv_win[:, 2 * QK :]
        stats = []
        for m in range(2):
            k_m = kv_win[:, m * QK : (m + 1) * QK]
            scores = jnp.einsum("qd,kd->qk", q_pair[:, m, :], k_m, preferred_element_type=jnp.float32) * scale
            scores = jnp.where(allowed, scores, masked_score)
            top = jnp.max(scores, axis=-1, keepdims=True)
            weights = jnp.where(allowed, jnp.exp(scores - top), 0.0)
            mass = jnp.sum(weights, axis=-1, keepdims=True)
            acc = jnp.dot(weights.astype(jnp.bfloat16), v_win, preferred_element_type=jnp.float32)
            stats.append((top, mass, acc))
        return stats

    all_stats = [part(p) for p in range(pieces)]

    def attend(m):
        tops = [stats[m][0] for stats in all_stats]
        top = tops[0]
        for other in tops[1:]:
            top = jnp.maximum(top, other)
        acc = 0.0
        mass = 0.0
        for stats in all_stats:
            fade = jnp.exp(stats[m][0] - top)
            mass = mass + stats[m][1] * fade
            acc = acc + stats[m][2] * fade
        return acc / mass

    lam_h = lax.dynamic_index_in_dim(lam, core, keepdims=False)
    gain_h = lax.dynamic_index_in_dim(sub_gain, core, axis=0, keepdims=False)
    diff = attend(0) - lam_h * attend(1)
    head_out = (
        diff * lax.rsqrt(jnp.mean(diff * diff, axis=-1, keepdims=True) + 1e-05) * gain_h * (1.0 - lambda_start)
    ).astype(jnp.bfloat16)
    own_rows = lax.dynamic_slice_in_dim(head_out, core * rows, rows, axis=0)
    other_rows = swap_cores(lax.dynamic_slice_in_dim(head_out, (1 - core) * rows, rows, axis=0))
    merged = jnp.where(
        core == 0,
        jnp.concatenate([own_rows, other_rows], axis=1),
        jnp.concatenate([other_rows, own_rows], axis=1),
    )
    summed = lax.psum(
        jnp.dot(merged, w_out, preferred_element_type=jnp.float32).astype(jnp.bfloat16), "tp"
    ).astype(jnp.float32)
    hidden = (xf + summed).astype(jnp.bfloat16)
    return (hidden, key_flat, values)


def solution(mesh):
    req, tp = mesh.shape["req"], mesh.shape["tp"]
    paired = Mesh(mesh.devices.reshape(req // 16, 2, 4, 2, tp), ("y", "z", "x", "core", "tp"))
    rows = ("y", "z", "x", "core")
    in_specs = (
        P(rows, None),
        P(),
        P(None, "tp"),
        P(None, "tp"),
        P(None, "tp"),
        P("tp", None),
        P(None, "tp", None),
        P("tp", None),
        P(),
    )
    out_specs = (P(rows, None), P(rows, "tp"), P(rows, "tp"))
    return jax.shard_map(
        on_device, mesh=paired, in_specs=in_specs, out_specs=out_specs, check_vma=False
    )
```

```python
import math

import jax
import jax.numpy as jnp
from jax import lax
from jax.sharding import Mesh
from jax.sharding import PartitionSpec as P

QK = 128
VD = 256
MAXLEN = 8192


lambda_start = 0.8 - 0.6 * math.exp(-3.3)
masked_score = -1e30


def locate(index, lengths):
    ends = jnp.cumsum(lengths)
    starts = ends - lengths
    segment = jnp.sum((ends[None, :] <= index[:, None]).astype(jnp.int32), axis=1)
    hit = jnp.arange(lengths.shape[0], dtype=jnp.int32)[None, :] == segment[:, None]
    begin = jnp.sum(jnp.where(hit, starts[None, :], 0), axis=1)
    return (segment, index - begin)


def rotate(proj, position):
    half = proj.shape[-1] // 2
    freq = 10000.0 ** (-jnp.arange(half, dtype=jnp.float32) / half)
    angle = position.astype(jnp.float32)[:, None] * freq[None, :]
    cosine = jnp.cos(angle)[:, None, None, :]
    sine = jnp.sin(angle)[:, None, None, :]
    front = proj[..., :half]
    back = proj[..., half:]
    return jnp.concatenate([front * cosine - back * sine, back * cosine + front * sine], axis=-1)


def swap_cores(value):
    return lax.ppermute(value, "core", [(0, 1), (1, 0)])


def on_device(tokens, norm_gain, w_query, w_key, w_value, w_out, lambdas, sub_gain, lengths):
    rows = tokens.shape[0]
    heads = w_query.shape[1] // (2 * QK)
    key_cols = heads * 2 * QK
    ys, zs, xs = lax.axis_size("y"), lax.axis_size("z"), lax.axis_size("x")
    chips = ys * zs * xs
    total = rows * 2 * chips
    core = lax.axis_index("core")
    chip = (lax.axis_index("y") * zs + lax.axis_index("z")) * xs + lax.axis_index("x")
    first = (chip * 2 + core) * rows
    local_index = first + jnp.arange(rows, dtype=jnp.int32)
    unused, pos_own = locate(local_index, lengths)
    xf = tokens.astype(jnp.float32)
    normed = (xf * lax.rsqrt(jnp.mean(xf * xf, axis=-1, keepdims=True) + 1e-06) * norm_gain).astype(
        jnp.bfloat16
    )
    keys = rotate(
        jnp.dot(normed, w_key, preferred_element_type=jnp.float32).reshape(rows, heads, 2, QK),
        pos_own,
    ).astype(jnp.bfloat16)
    values = jnp.dot(normed, w_value, preferred_element_type=jnp.float32).astype(jnp.bfloat16)
    key_flat = keys.reshape(rows, key_cols)
    lam = (
        jnp.exp(jnp.sum(lambdas[0] * lambdas[1], axis=-1))
        - jnp.exp(jnp.sum(lambdas[2] * lambdas[3], axis=-1))
        + lambda_start
    )
    scale = QK ** (-0.5)

    def head_kv(h):
        k_h = lax.dynamic_index_in_dim(keys, h, axis=1, keepdims=False).reshape(rows, 2 * QK)
        v_h = lax.dynamic_index_in_dim(values.reshape(rows, heads, VD), h, axis=1, keepdims=False)
        return jnp.concatenate([k_h, v_h], axis=1)

    def in_order(mine, theirs, first_is_mine):
        rows_each = mine.shape[0]
        both = jnp.zeros((2 * rows_each,) + mine.shape[1:], mine.dtype)
        both = lax.dynamic_update_slice_in_dim(both, mine, jnp.where(first_is_mine, 0, rows_each), axis=0)
        return lax.dynamic_update_slice_in_dim(both, theirs, jnp.where(first_is_mine, rows_each, 0), axis=0)

    span = 2 * rows
    kv_pair = in_order(head_kv(core), swap_cores(head_kv(1 - core)), core == 0)
    z = lax.axis_index("z")
    kv_z = lax.ppermute(kv_pair, "z", [(0, 1), (1, 0)])
    kv_quad = in_order(kv_pair, kv_z, z == 0)
    gathered = lax.all_gather(kv_quad, ("y", "x"), axis=0, tiled=True)
    query = rotate(
        jnp.dot(normed, w_query, preferred_element_type=jnp.float32).reshape(rows, heads, 2, QK),
        pos_own,
    ).astype(jnp.bfloat16)
    q_pair = in_order(
        lax.dynamic_index_in_dim(query, core, axis=1, keepdims=False),
        swap_cores(lax.dynamic_index_in_dim(query, 1 - core, axis=1, keepdims=False)),
        core == 0,
    )

    reach = min(MAXLEN // span + 1, chips)
    window = reach * span
    base = chip * span
    first_chip = jnp.clip(chip + 1 - reach, 0, chips - reach)
    start = first_chip * span
    c = first_chip + jnp.arange(reach, dtype=jnp.int32)
    slot = ((c // (zs * xs)) * xs + c % xs) * zs + (c // xs) % zs
    kv_window = jnp.take(gathered.reshape(chips, span, -1), slot, axis=0, mode="clip").reshape(window, -1)
    q_index = base + jnp.arange(span, dtype=jnp.int32)
    q_seg, unused = locate(q_index, lengths)
    pieces = 4
    piece = window // pieces

    def absorb(p, carry):
        key_index = start + p * piece + jnp.arange(piece, dtype=jnp.int32)
        k_seg, unused = locate(key_index, lengths)
        allowed = (key_index[None, :] <= q_index[:, None]) & (k_seg[None, :] == q_seg[:, None])
        kv_win = lax.dynamic_slice_in_dim(kv_window, p * piece, piece, axis=0)
        v_win = kv_win[:, 2 * QK :]
        updated = []
        for m in range(2):
            top, mass, acc = carry[m]
            k_m = kv_win[:, m * QK : (m + 1) * QK]
            scores = jnp.einsum("qd,kd->qk", q_pair[:, m, :], k_m, preferred_element_type=jnp.float32) * scale
            scores = jnp.where(allowed, scores, masked_score)
            new_top = jnp.maximum(top, jnp.max(scores, axis=-1, keepdims=True))
            weights = jnp.where(allowed, jnp.exp(scores - new_top), 0.0)
            fade = jnp.exp(top - new_top)
            mass = mass * fade + jnp.sum(weights, axis=-1, keepdims=True)
            acc = acc * fade + jnp.dot(weights.astype(jnp.bfloat16), v_win, preferred_element_type=jnp.float32)
            updated.append((new_top, mass, acc))
        return tuple(updated)

    empty = (
        jnp.full((span, 1), masked_score, jnp.float32),
        jnp.zeros((span, 1), jnp.float32),
        jnp.zeros((span, VD), jnp.float32),
    )
    final = lax.fori_loop(0, pieces, absorb, (empty, empty))

    def attend(m):
        top, mass, acc = final[m]
        return acc / mass

    lam_h = lax.dynamic_index_in_dim(lam, core, keepdims=False)
    gain_h = lax.dynamic_index_in_dim(sub_gain, core, axis=0, keepdims=False)
    diff = attend(0) - lam_h * attend(1)
    head_out = (
        diff * lax.rsqrt(jnp.mean(diff * diff, axis=-1, keepdims=True) + 1e-05) * gain_h * (1.0 - lambda_start)
    ).astype(jnp.bfloat16)
    own_rows = lax.dynamic_slice_in_dim(head_out, core * rows, rows, axis=0)
    other_rows = swap_cores(lax.dynamic_slice_in_dim(head_out, (1 - core) * rows, rows, axis=0))
    merged = jnp.where(
        core == 0,
        jnp.concatenate([own_rows, other_rows], axis=1),
        jnp.concatenate([other_rows, own_rows], axis=1),
    )
    summed = lax.psum(
        jnp.dot(merged, w_out, preferred_element_type=jnp.float32).astype(jnp.bfloat16), "tp"
    ).astype(jnp.float32)
    hidden = (xf + summed).astype(jnp.bfloat16)
    return (hidden, key_flat, values)


def solution(mesh):
    req, tp = mesh.shape["req"], mesh.shape["tp"]
    paired = Mesh(mesh.devices.reshape(req // 16, 2, 4, 2, tp), ("y", "z", "x", "core", "tp"))
    rows = ("y", "z", "x", "core")
    in_specs = (
        P(rows, None),
        P(),
        P(None, "tp"),
        P(None, "tp"),
        P(None, "tp"),
        P("tp", None),
        P(None, "tp", None),
        P("tp", None),
        P(),
    )
    out_specs = (P(rows, None), P(rows, "tp"), P(rows, "tp"))
    return jax.shard_map(
        on_device, mesh=paired, in_specs=in_specs, out_specs=out_specs, check_vma=False
    )
```

```python
import math

import jax
import jax.numpy as jnp
from jax import lax
from jax.sharding import Mesh
from jax.sharding import PartitionSpec as P

QK = 128
VD = 256
MAXLEN = 8192


lambda_start = 0.8 - 0.6 * math.exp(-3.3)
masked_score = -1e30


def locate(index, lengths):
    ends = jnp.cumsum(lengths)
    starts = ends - lengths
    segment = jnp.sum((ends[None, :] <= index[:, None]).astype(jnp.int32), axis=1)
    hit = jnp.arange(lengths.shape[0], dtype=jnp.int32)[None, :] == segment[:, None]
    begin = jnp.sum(jnp.where(hit, starts[None, :], 0), axis=1)
    return (segment, index - begin)


def rotate(proj, position):
    half = proj.shape[-1] // 2
    freq = 10000.0 ** (-jnp.arange(half, dtype=jnp.float32) / half)
    angle = position.astype(jnp.float32)[:, None] * freq[None, :]
    cosine = jnp.cos(angle)[:, None, None, :]
    sine = jnp.sin(angle)[:, None, None, :]
    front = proj[..., :half]
    back = proj[..., half:]
    return jnp.concatenate([front * cosine - back * sine, back * cosine + front * sine], axis=-1)


def swap_cores(value):
    return lax.ppermute(value, "core", [(0, 1), (1, 0)])


def on_device(tokens, norm_gain, w_query, w_key, w_value, w_out, lambdas, sub_gain, lengths):
    rows = tokens.shape[0]
    heads = w_query.shape[1] // (2 * QK)
    key_cols = heads * 2 * QK
    ys, zs, xs = lax.axis_size("y"), lax.axis_size("z"), lax.axis_size("x")
    chips = ys * zs * xs
    total = rows * 2 * chips
    core = lax.axis_index("core")
    chip = (lax.axis_index("y") * zs + lax.axis_index("z")) * xs + lax.axis_index("x")
    first = (chip * 2 + core) * rows
    local_index = first + jnp.arange(rows, dtype=jnp.int32)
    unused, pos_own = locate(local_index, lengths)
    xf = tokens.astype(jnp.float32)
    normed = (xf * lax.rsqrt(jnp.mean(xf * xf, axis=-1, keepdims=True) + 1e-06) * norm_gain).astype(
        jnp.bfloat16
    )
    keys = rotate(
        jnp.dot(normed, w_key, preferred_element_type=jnp.float32).reshape(rows, heads, 2, QK),
        pos_own,
    ).astype(jnp.bfloat16)
    values = jnp.dot(normed, w_value, preferred_element_type=jnp.float32).astype(jnp.bfloat16)
    key_flat = keys.reshape(rows, key_cols)
    lam = (
        jnp.exp(jnp.sum(lambdas[0] * lambdas[1], axis=-1))
        - jnp.exp(jnp.sum(lambdas[2] * lambdas[3], axis=-1))
        + lambda_start
    )
    scale = QK ** (-0.5)

    def head_kv(h):
        k_h = lax.dynamic_index_in_dim(keys, h, axis=1, keepdims=False).reshape(rows, 2 * QK)
        v_h = lax.dynamic_index_in_dim(values.reshape(rows, heads, VD), h, axis=1, keepdims=False)
        return jnp.concatenate([k_h, v_h], axis=1)

    def in_order(mine, theirs, first_is_mine):
        rows_each = mine.shape[0]
        both = jnp.zeros((2 * rows_each,) + mine.shape[1:], mine.dtype)
        both = lax.dynamic_update_slice_in_dim(both, mine, jnp.where(first_is_mine, 0, rows_each), axis=0)
        return lax.dynamic_update_slice_in_dim(both, theirs, jnp.where(first_is_mine, rows_each, 0), axis=0)

    span = 2 * rows
    kv_pair = in_order(head_kv(core), swap_cores(head_kv(1 - core)), core == 0)
    z = lax.axis_index("z")
    kv_z = lax.ppermute(kv_pair, "z", [(0, 1), (1, 0)])
    kv_quad = in_order(kv_pair, kv_z, z == 0)
    gathered = lax.all_gather(kv_quad, ("y", "x"), axis=0, tiled=True)
    query = rotate(
        jnp.dot(normed, w_query, preferred_element_type=jnp.float32).reshape(rows, heads, 2, QK),
        pos_own,
    ).astype(jnp.bfloat16)
    q_pair = in_order(
        lax.dynamic_index_in_dim(query, core, axis=1, keepdims=False),
        swap_cores(lax.dynamic_index_in_dim(query, 1 - core, axis=1, keepdims=False)),
        core == 0,
    )

    reach = min(MAXLEN // span + 1, chips)
    window = reach * span
    base = chip * span
    first_chip = jnp.clip(chip + 1 - reach, 0, chips - reach)
    start = first_chip * span
    c = first_chip + jnp.arange(reach, dtype=jnp.int32)
    slot = ((c // (zs * xs)) * xs + c % xs) * zs + (c // xs) % zs
    kv_window = jnp.take(gathered.reshape(chips, span, -1), slot, axis=0, mode="clip").reshape(window, -1)
    q_index = base + jnp.arange(span, dtype=jnp.int32)
    q_seg, unused = locate(q_index, lengths)
    pieces = 2
    piece = window // pieces

    def part(p):
        key_index = start + p * piece + jnp.arange(piece, dtype=jnp.int32)
        k_seg, unused = locate(key_index, lengths)
        allowed = (key_index[None, :] <= q_index[:, None]) & (k_seg[None, :] == q_seg[:, None])
        kv_win = kv_window[p * piece : (p + 1) * piece]
        v_win = kv_win[:, 2 * QK :]
        stats = []
        for m in range(2):
            k_m = kv_win[:, m * QK : (m + 1) * QK]
            scores = jnp.einsum("qd,kd->qk", q_pair[:, m, :], k_m, preferred_element_type=jnp.float32) * scale
            scores = jnp.where(allowed, scores, masked_score)
            top = jnp.max(scores, axis=-1, keepdims=True)
            weights = jnp.where(allowed, jnp.exp(scores - top), 0.0)
            mass = jnp.sum(weights, axis=-1, keepdims=True)
            acc = jnp.dot(weights.astype(jnp.bfloat16), v_win, preferred_element_type=jnp.float32)
            stats.append((top, mass, acc))
        return stats

    all_stats = [part(p) for p in range(pieces)]

    def attend(m):
        tops = [stats[m][0] for stats in all_stats]
        top = tops[0]
        for other in tops[1:]:
            top = jnp.maximum(top, other)
        acc = 0.0
        mass = 0.0
        for stats in all_stats:
            fade = jnp.exp(stats[m][0] - top)
            mass = mass + stats[m][1] * fade
            acc = acc + stats[m][2] * fade
        return acc / mass

    lam_h = lax.dynamic_index_in_dim(lam, core, keepdims=False)
    gain_h = lax.dynamic_index_in_dim(sub_gain, core, axis=0, keepdims=False)
    diff = attend(0) - lam_h * attend(1)
    head_out = (
        diff * lax.rsqrt(jnp.mean(diff * diff, axis=-1, keepdims=True) + 1e-05) * gain_h * (1.0 - lambda_start)
    ).astype(jnp.bfloat16)
    own_rows = lax.dynamic_slice_in_dim(head_out, core * rows, rows, axis=0)
    other_rows = swap_cores(lax.dynamic_slice_in_dim(head_out, (1 - core) * rows, rows, axis=0))
    merged = jnp.where(
        core == 0,
        jnp.concatenate([own_rows, other_rows], axis=1),
        jnp.concatenate([other_rows, own_rows], axis=1),
    )
    summed = lax.psum(
        jnp.dot(merged, w_out, preferred_element_type=jnp.float32).astype(jnp.bfloat16), "tp"
    ).astype(jnp.float32)
    hidden = (xf + summed).astype(jnp.bfloat16)
    return (hidden, key_flat, values)


def solution(mesh):
    req, tp = mesh.shape["req"], mesh.shape["tp"]
    paired = Mesh(mesh.devices.reshape(req // 16, 2, 4, 2, tp), ("y", "z", "x", "core", "tp"))
    rows = ("y", "z", "x", "core")
    in_specs = (
        P(rows, None),
        P(),
        P(None, "tp"),
        P(None, "tp"),
        P(None, "tp"),
        P("tp", None),
        P(None, "tp", None),
        P("tp", None),
        P(),
    )
    out_specs = (P(rows, None), P(rows, "tp"), P(rows, "tp"))
    return jax.shard_map(
        on_device, mesh=paired, in_specs=in_specs, out_specs=out_specs, check_vma=False
    )
```

```python
import math

import jax
import jax.numpy as jnp
from jax import lax
from jax.sharding import Mesh
from jax.sharding import PartitionSpec as P

QK = 128
VD = 256
MAXLEN = 8192


lambda_start = 0.8 - 0.6 * math.exp(-3.3)
masked_score = -1e30


def locate(index, lengths):
    ends = jnp.cumsum(lengths)
    starts = ends - lengths
    segment = jnp.sum((ends[None, :] <= index[:, None]).astype(jnp.int32), axis=1)
    hit = jnp.arange(lengths.shape[0], dtype=jnp.int32)[None, :] == segment[:, None]
    begin = jnp.sum(jnp.where(hit, starts[None, :], 0), axis=1)
    return (segment, index - begin)


def rotate(proj, position):
    half = proj.shape[-1] // 2
    freq = 10000.0 ** (-jnp.arange(half, dtype=jnp.float32) / half)
    angle = position.astype(jnp.float32)[:, None] * freq[None, :]
    cosine = jnp.cos(angle)[:, None, None, :]
    sine = jnp.sin(angle)[:, None, None, :]
    front = proj[..., :half]
    back = proj[..., half:]
    return jnp.concatenate([front * cosine - back * sine, back * cosine + front * sine], axis=-1)


def swap_cores(value):
    return lax.ppermute(value, "core", [(0, 1), (1, 0)])


def on_device(tokens, norm_gain, w_query, w_key, w_value, w_out, lambdas, sub_gain, lengths):
    rows = tokens.shape[0]
    heads = w_query.shape[1] // (2 * QK)
    key_cols = heads * 2 * QK
    ys, zs, xs = lax.axis_size("y"), lax.axis_size("z"), lax.axis_size("x")
    chips = ys * zs * xs
    total = rows * 2 * chips
    core = lax.axis_index("core")
    chip = (lax.axis_index("y") * zs + lax.axis_index("z")) * xs + lax.axis_index("x")
    first = (chip * 2 + core) * rows
    local_index = first + jnp.arange(rows, dtype=jnp.int32)
    unused, pos_own = locate(local_index, lengths)
    xf = tokens.astype(jnp.float32)
    normed = (xf * lax.rsqrt(jnp.mean(xf * xf, axis=-1, keepdims=True) + 1e-06) * norm_gain).astype(
        jnp.bfloat16
    )
    keys = rotate(
        jnp.dot(normed, w_key, preferred_element_type=jnp.float32).reshape(rows, heads, 2, QK),
        pos_own,
    ).astype(jnp.bfloat16)
    values = jnp.dot(normed, w_value, preferred_element_type=jnp.float32).astype(jnp.bfloat16)
    key_flat = keys.reshape(rows, key_cols)
    lam = (
        jnp.exp(jnp.sum(lambdas[0] * lambdas[1], axis=-1))
        - jnp.exp(jnp.sum(lambdas[2] * lambdas[3], axis=-1))
        + lambda_start
    )
    scale = QK ** (-0.5)

    def head_kv(h):
        k_h = lax.dynamic_index_in_dim(keys, h, axis=1, keepdims=False).reshape(rows, 2 * QK)
        v_h = lax.dynamic_index_in_dim(values.reshape(rows, heads, VD), h, axis=1, keepdims=False)
        return jnp.concatenate([k_h, v_h], axis=1)

    def in_order(mine, theirs, first_is_mine):
        rows_each = mine.shape[0]
        both = jnp.zeros((2 * rows_each,) + mine.shape[1:], mine.dtype)
        both = lax.dynamic_update_slice_in_dim(both, mine, jnp.where(first_is_mine, 0, rows_each), axis=0)
        return lax.dynamic_update_slice_in_dim(both, theirs, jnp.where(first_is_mine, rows_each, 0), axis=0)

    span = 2 * rows
    kv_pair = in_order(head_kv(core), swap_cores(head_kv(1 - core)), core == 0)
    z = lax.axis_index("z")
    kv_z = lax.ppermute(kv_pair, "z", [(0, 1), (1, 0)])
    kv_quad = in_order(kv_pair, kv_z, z == 0)
    gathered = lax.all_gather(kv_quad, ("y", "x"), axis=0, tiled=True)
    query = rotate(
        jnp.dot(normed, w_query, preferred_element_type=jnp.float32).reshape(rows, heads, 2, QK),
        pos_own,
    ).astype(jnp.bfloat16)
    q_pair = in_order(
        lax.dynamic_index_in_dim(query, core, axis=1, keepdims=False),
        swap_cores(lax.dynamic_index_in_dim(query, 1 - core, axis=1, keepdims=False)),
        core == 0,
    )

    reach = min(MAXLEN // span, chips - 1)
    window = reach * span
    base = chip * span
    first_chip = jnp.clip(chip - reach, 0, chips - reach)
    start = first_chip * span
    q_index = base + jnp.arange(span, dtype=jnp.int32)
    q_seg, unused = locate(q_index, lengths)

    def stats_of(kv_win, key_index, allowed):
        v_win = kv_win[:, 2 * QK :]
        stats = []
        for m in range(2):
            k_m = kv_win[:, m * QK : (m + 1) * QK]
            scores = jnp.einsum("qd,kd->qk", q_pair[:, m, :], k_m, preferred_element_type=jnp.float32) * scale
            scores = jnp.where(allowed, scores, masked_score)
            top = jnp.max(scores, axis=-1, keepdims=True)
            weights = jnp.where(allowed, jnp.exp(scores - top), 0.0)
            mass = jnp.sum(weights, axis=-1, keepdims=True)
            acc = jnp.dot(weights.astype(jnp.bfloat16), v_win, preferred_element_type=jnp.float32)
            stats.append((top, mass, acc))
        return stats

    local_allowed = (q_index[None, :] <= q_index[:, None]) & (q_seg[None, :] == q_seg[:, None])
    local_stats = stats_of(kv_pair, q_index, local_allowed)
    local_stats, gathered = lax.optimization_barrier((local_stats, gathered))

    c = first_chip + jnp.arange(reach, dtype=jnp.int32)
    slot = ((c // (zs * xs)) * xs + c % xs) * zs + (c // xs) % zs
    kv_window = jnp.take(gathered.reshape(chips, span, -1), slot, axis=0, mode="clip").reshape(window, -1)
    pieces = 2
    piece = window // pieces

    def part(p):
        key_index = start + p * piece + jnp.arange(piece, dtype=jnp.int32)
        k_seg, unused = locate(key_index, lengths)
        allowed = (key_index[None, :] < base) & (k_seg[None, :] == q_seg[:, None])
        return stats_of(kv_window[p * piece : (p + 1) * piece], key_index, allowed)

    all_stats = [local_stats] + [part(p) for p in range(pieces)]

    def attend(m):
        tops = [stats[m][0] for stats in all_stats]
        top = tops[0]
        for other in tops[1:]:
            top = jnp.maximum(top, other)
        acc = 0.0
        mass = 0.0
        for stats in all_stats:
            fade = jnp.exp(stats[m][0] - top)
            mass = mass + stats[m][1] * fade
            acc = acc + stats[m][2] * fade
        return acc / mass

    lam_h = lax.dynamic_index_in_dim(lam, core, keepdims=False)
    gain_h = lax.dynamic_index_in_dim(sub_gain, core, axis=0, keepdims=False)
    diff = attend(0) - lam_h * attend(1)
    head_out = (
        diff * lax.rsqrt(jnp.mean(diff * diff, axis=-1, keepdims=True) + 1e-05) * gain_h * (1.0 - lambda_start)
    ).astype(jnp.bfloat16)
    own_rows = lax.dynamic_slice_in_dim(head_out, core * rows, rows, axis=0)
    other_rows = swap_cores(lax.dynamic_slice_in_dim(head_out, (1 - core) * rows, rows, axis=0))
    merged = jnp.where(
        core == 0,
        jnp.concatenate([own_rows, other_rows], axis=1),
        jnp.concatenate([other_rows, own_rows], axis=1),
    )
    summed = lax.psum(
        jnp.dot(merged, w_out, preferred_element_type=jnp.float32).astype(jnp.bfloat16), "tp"
    ).astype(jnp.float32)
    hidden = (xf + summed).astype(jnp.bfloat16)
    return (hidden, key_flat, values)


def solution(mesh):
    req, tp = mesh.shape["req"], mesh.shape["tp"]
    paired = Mesh(mesh.devices.reshape(req // 16, 2, 4, 2, tp), ("y", "z", "x", "core", "tp"))
    rows = ("y", "z", "x", "core")
    in_specs = (
        P(rows, None),
        P(),
        P(None, "tp"),
        P(None, "tp"),
        P(None, "tp"),
        P("tp", None),
        P(None, "tp", None),
        P("tp", None),
        P(),
    )
    out_specs = (P(rows, None), P(rows, "tp"), P(rows, "tp"))
    return jax.shard_map(
        on_device, mesh=paired, in_specs=in_specs, out_specs=out_specs, check_vma=False
    )
```

```python
import math

import jax
import jax.numpy as jnp
from jax import lax
from jax.sharding import Mesh
from jax.sharding import PartitionSpec as P

QK = 128
VD = 256
MAXLEN = 8192


lambda_start = 0.8 - 0.6 * math.exp(-3.3)
masked_score = -1e30


def locate(index, lengths):
    ends = jnp.cumsum(lengths)
    starts = ends - lengths
    segment = jnp.sum((ends[None, :] <= index[:, None]).astype(jnp.int32), axis=1)
    hit = jnp.arange(lengths.shape[0], dtype=jnp.int32)[None, :] == segment[:, None]
    begin = jnp.sum(jnp.where(hit, starts[None, :], 0), axis=1)
    return (segment, index - begin)


def rotate(proj, position):
    half = proj.shape[-1] // 2
    freq = 10000.0 ** (-jnp.arange(half, dtype=jnp.float32) / half)
    angle = position.astype(jnp.float32)[:, None] * freq[None, :]
    cosine = jnp.cos(angle)[:, None, None, :]
    sine = jnp.sin(angle)[:, None, None, :]
    front = proj[..., :half]
    back = proj[..., half:]
    return jnp.concatenate([front * cosine - back * sine, back * cosine + front * sine], axis=-1)


def swap_cores(value):
    return lax.ppermute(value, "core", [(0, 1), (1, 0)])


def on_device(tokens, norm_gain, w_query, w_key, w_value, w_out, lambdas, sub_gain, lengths):
    rows = tokens.shape[0]
    heads = w_query.shape[1] // (2 * QK)
    key_cols = heads * 2 * QK
    ys, zs, xs = lax.axis_size("y"), lax.axis_size("z"), lax.axis_size("x")
    chips = ys * zs * xs
    total = rows * 2 * chips
    core = lax.axis_index("core")
    chip = (lax.axis_index("y") * zs + lax.axis_index("z")) * xs + lax.axis_index("x")
    first = (chip * 2 + core) * rows
    local_index = first + jnp.arange(rows, dtype=jnp.int32)
    unused, pos_own = locate(local_index, lengths)
    xf = tokens.astype(jnp.float32)
    normed = (xf * lax.rsqrt(jnp.mean(xf * xf, axis=-1, keepdims=True) + 1e-06) * norm_gain).astype(
        jnp.bfloat16
    )
    keys = rotate(
        jnp.dot(normed, w_key, preferred_element_type=jnp.float32).reshape(rows, heads, 2, QK),
        pos_own,
    ).astype(jnp.bfloat16)
    values = jnp.dot(normed, w_value, preferred_element_type=jnp.float32).astype(jnp.bfloat16)
    key_flat = keys.reshape(rows, key_cols)
    lam = (
        jnp.exp(jnp.sum(lambdas[0] * lambdas[1], axis=-1))
        - jnp.exp(jnp.sum(lambdas[2] * lambdas[3], axis=-1))
        + lambda_start
    )
    scale = QK ** (-0.5)

    def head_kv(h):
        k_h = lax.dynamic_index_in_dim(keys, h, axis=1, keepdims=False).reshape(rows, 2 * QK)
        v_h = lax.dynamic_index_in_dim(values.reshape(rows, heads, VD), h, axis=1, keepdims=False)
        return jnp.concatenate([k_h, v_h], axis=1)

    def in_order(mine, theirs, first_is_mine):
        rows_each = mine.shape[0]
        both = jnp.zeros((2 * rows_each,) + mine.shape[1:], mine.dtype)
        both = lax.dynamic_update_slice_in_dim(both, mine, jnp.where(first_is_mine, 0, rows_each), axis=0)
        return lax.dynamic_update_slice_in_dim(both, theirs, jnp.where(first_is_mine, rows_each, 0), axis=0)

    span = 2 * rows
    kv_pair = in_order(head_kv(core), swap_cores(head_kv(1 - core)), core == 0)
    z = lax.axis_index("z")
    kv_z = lax.ppermute(kv_pair, "z", [(0, 1), (1, 0)])
    kv_quad = in_order(kv_pair, kv_z, z == 0)
    gathered = lax.all_gather(kv_quad, ("y", "x"), axis=0, tiled=True)
    query = rotate(
        jnp.dot(normed, w_query, preferred_element_type=jnp.float32).reshape(rows, heads, 2, QK),
        pos_own,
    ).astype(jnp.bfloat16)
    q_pair = in_order(
        lax.dynamic_index_in_dim(query, core, axis=1, keepdims=False),
        swap_cores(lax.dynamic_index_in_dim(query, 1 - core, axis=1, keepdims=False)),
        core == 0,
    )

    reach = min(MAXLEN // span, chips - 1)
    window = reach * span
    base = chip * span
    first_chip = jnp.clip(chip - reach, 0, chips - reach)
    start = first_chip * span
    q_index = base + jnp.arange(span, dtype=jnp.int32)
    q_seg, unused = locate(q_index, lengths)

    def stats_of(kv_win, key_index, allowed):
        v_win = kv_win[:, 2 * QK :]
        stats = []
        for m in range(2):
            k_m = kv_win[:, m * QK : (m + 1) * QK]
            scores = jnp.einsum("qd,kd->qk", q_pair[:, m, :], k_m, preferred_element_type=jnp.float32) * scale
            scores = jnp.where(allowed, scores, masked_score)
            top = jnp.max(scores, axis=-1, keepdims=True)
            weights = jnp.where(allowed, jnp.exp(scores - top), 0.0)
            mass = jnp.sum(weights, axis=-1, keepdims=True)
            acc = jnp.dot(weights.astype(jnp.bfloat16), v_win, preferred_element_type=jnp.float32)
            stats.append((top, mass, acc))
        return stats

    local_allowed = (q_index[None, :] <= q_index[:, None]) & (q_seg[None, :] == q_seg[:, None])
    local_stats = stats_of(kv_pair, q_index, local_allowed)
    local_stats, gathered = lax.optimization_barrier((local_stats, gathered))

    c = first_chip + jnp.arange(reach, dtype=jnp.int32)
    slot = ((c // (zs * xs)) * xs + c % xs) * zs + (c // xs) % zs
    pieces = 2
    piece = window // pieces
    per_piece = reach // pieces
    chip_blocks = gathered.reshape(chips, span, -1)

    def part(p):
        key_index = start + p * piece + jnp.arange(piece, dtype=jnp.int32)
        k_seg, unused = locate(key_index, lengths)
        allowed = (key_index[None, :] < base) & (k_seg[None, :] == q_seg[:, None])
        kv_piece = jnp.take(chip_blocks, slot[p * per_piece : (p + 1) * per_piece], axis=0, mode="clip")
        return stats_of(kv_piece.reshape(piece, -1), key_index, allowed)

    all_stats = [local_stats] + [part(p) for p in range(pieces)]

    def attend(m):
        tops = [stats[m][0] for stats in all_stats]
        top = tops[0]
        for other in tops[1:]:
            top = jnp.maximum(top, other)
        acc = 0.0
        mass = 0.0
        for stats in all_stats:
            fade = jnp.exp(stats[m][0] - top)
            mass = mass + stats[m][1] * fade
            acc = acc + stats[m][2] * fade
        return acc / mass

    lam_h = lax.dynamic_index_in_dim(lam, core, keepdims=False)
    gain_h = lax.dynamic_index_in_dim(sub_gain, core, axis=0, keepdims=False)
    diff = attend(0) - lam_h * attend(1)
    head_out = (
        diff * lax.rsqrt(jnp.mean(diff * diff, axis=-1, keepdims=True) + 1e-05) * gain_h * (1.0 - lambda_start)
    ).astype(jnp.bfloat16)
    own_rows = lax.dynamic_slice_in_dim(head_out, core * rows, rows, axis=0)
    other_rows = swap_cores(lax.dynamic_slice_in_dim(head_out, (1 - core) * rows, rows, axis=0))
    merged = jnp.where(
        core == 0,
        jnp.concatenate([own_rows, other_rows], axis=1),
        jnp.concatenate([other_rows, own_rows], axis=1),
    )
    summed = lax.psum(
        jnp.dot(merged, w_out, preferred_element_type=jnp.float32).astype(jnp.bfloat16), "tp"
    ).astype(jnp.float32)
    hidden = (xf + summed).astype(jnp.bfloat16)
    return (hidden, key_flat, values)


def solution(mesh):
    req, tp = mesh.shape["req"], mesh.shape["tp"]
    paired = Mesh(mesh.devices.reshape(req // 16, 2, 4, 2, tp), ("y", "z", "x", "core", "tp"))
    rows = ("y", "z", "x", "core")
    in_specs = (
        P(rows, None),
        P(),
        P(None, "tp"),
        P(None, "tp"),
        P(None, "tp"),
        P("tp", None),
        P(None, "tp", None),
        P("tp", None),
        P(),
    )
    out_specs = (P(rows, None), P(rows, "tp"), P(rows, "tp"))
    return jax.shard_map(
        on_device, mesh=paired, in_specs=in_specs, out_specs=out_specs, check_vma=False
    )
```

```python
import math

import jax
import jax.numpy as jnp
from jax import lax
from jax.sharding import Mesh
from jax.sharding import PartitionSpec as P

QK = 128
VD = 256
MAXLEN = 8192


lambda_start = 0.8 - 0.6 * math.exp(-3.3)
masked_score = -1e30


def locate(index, lengths):
    ends = jnp.cumsum(lengths)
    starts = ends - lengths
    segment = jnp.sum((ends[None, :] <= index[:, None]).astype(jnp.int32), axis=1)
    hit = jnp.arange(lengths.shape[0], dtype=jnp.int32)[None, :] == segment[:, None]
    begin = jnp.sum(jnp.where(hit, starts[None, :], 0), axis=1)
    return (segment, index - begin)


def rotate(proj, position):
    half = proj.shape[-1] // 2
    freq = 10000.0 ** (-jnp.arange(half, dtype=jnp.float32) / half)
    angle = position.astype(jnp.float32)[:, None] * freq[None, :]
    cosine = jnp.cos(angle)[:, None, None, :]
    sine = jnp.sin(angle)[:, None, None, :]
    front = proj[..., :half]
    back = proj[..., half:]
    return jnp.concatenate([front * cosine - back * sine, back * cosine + front * sine], axis=-1)


def swap_cores(value):
    return lax.ppermute(value, "core", [(0, 1), (1, 0)])


def on_device(tokens, norm_gain, w_query, w_key, w_value, w_out, lambdas, sub_gain, lengths):
    rows = tokens.shape[0]
    heads = w_query.shape[1] // (2 * QK)
    key_cols = heads * 2 * QK
    ys, zs, xs = lax.axis_size("y"), lax.axis_size("z"), lax.axis_size("x")
    chips = ys * zs * xs
    total = rows * 2 * chips
    core = lax.axis_index("core")
    chip = (lax.axis_index("y") * zs + lax.axis_index("z")) * xs + lax.axis_index("x")
    first = (chip * 2 + core) * rows
    local_index = first + jnp.arange(rows, dtype=jnp.int32)
    unused, pos_own = locate(local_index, lengths)
    xf = tokens.astype(jnp.float32)
    normed = (xf * lax.rsqrt(jnp.mean(xf * xf, axis=-1, keepdims=True) + 1e-06) * norm_gain).astype(
        jnp.bfloat16
    )
    keys = rotate(
        jnp.dot(normed, w_key, preferred_element_type=jnp.float32).reshape(rows, heads, 2, QK),
        pos_own,
    ).astype(jnp.bfloat16)
    values = jnp.dot(normed, w_value, preferred_element_type=jnp.float32).astype(jnp.bfloat16)
    key_flat = keys.reshape(rows, key_cols)
    lam = (
        jnp.exp(jnp.sum(lambdas[0] * lambdas[1], axis=-1))
        - jnp.exp(jnp.sum(lambdas[2] * lambdas[3], axis=-1))
        + lambda_start
    )
    scale = QK ** (-0.5)

    def head_kv(h):
        k_h = lax.dynamic_index_in_dim(keys, h, axis=1, keepdims=False).reshape(rows, 2 * QK)
        v_h = lax.dynamic_index_in_dim(values.reshape(rows, heads, VD), h, axis=1, keepdims=False)
        return jnp.concatenate([k_h, v_h], axis=1)

    def in_order(mine, theirs, first_is_mine):
        rows_each = mine.shape[0]
        both = jnp.zeros((2 * rows_each,) + mine.shape[1:], mine.dtype)
        both = lax.dynamic_update_slice_in_dim(both, mine, jnp.where(first_is_mine, 0, rows_each), axis=0)
        return lax.dynamic_update_slice_in_dim(both, theirs, jnp.where(first_is_mine, rows_each, 0), axis=0)

    span = 2 * rows
    z = lax.axis_index("z")
    kv_both = jnp.stack([head_kv(0), head_kv(1)], axis=1)
    kv_chips = in_order(kv_both, lax.ppermute(kv_both, "z", [(0, 1), (1, 0)]), z == 0)
    mine = lax.dynamic_index_in_dim(kv_chips, core, axis=1, keepdims=False).reshape(2, rows, -1)
    theirs = swap_cores(lax.dynamic_index_in_dim(kv_chips, 1 - core, axis=1, keepdims=False)).reshape(2, rows, -1)
    quad = jnp.zeros((2, span, mine.shape[-1]), mine.dtype)
    quad = lax.dynamic_update_slice_in_dim(quad, mine, core * rows, axis=1)
    quad = lax.dynamic_update_slice_in_dim(quad, theirs, (1 - core) * rows, axis=1)
    kv_quad = quad.reshape(2 * span, -1)
    kv_pair = lax.dynamic_index_in_dim(quad, z, axis=0, keepdims=False)
    gathered = lax.all_gather(kv_quad, ("y", "x"), axis=0, tiled=True)
    query = rotate(
        jnp.dot(normed, w_query, preferred_element_type=jnp.float32).reshape(rows, heads, 2, QK),
        pos_own,
    ).astype(jnp.bfloat16)
    q_pair = in_order(
        lax.dynamic_index_in_dim(query, core, axis=1, keepdims=False),
        swap_cores(lax.dynamic_index_in_dim(query, 1 - core, axis=1, keepdims=False)),
        core == 0,
    )

    reach = min(MAXLEN // span, chips - 1)
    window = reach * span
    base = chip * span
    first_chip = jnp.clip(chip - reach, 0, chips - reach)
    start = first_chip * span
    q_index = base + jnp.arange(span, dtype=jnp.int32)
    q_seg, unused = locate(q_index, lengths)

    def stats_of(kv_win, key_index, allowed):
        v_win = kv_win[:, 2 * QK :]
        stats = []
        for m in range(2):
            k_m = kv_win[:, m * QK : (m + 1) * QK]
            scores = jnp.einsum("qd,kd->qk", q_pair[:, m, :], k_m, preferred_element_type=jnp.float32) * scale
            scores = jnp.where(allowed, scores, masked_score)
            top = jnp.max(scores, axis=-1, keepdims=True)
            weights = jnp.where(allowed, jnp.exp(scores - top), 0.0)
            mass = jnp.sum(weights, axis=-1, keepdims=True)
            acc = jnp.dot(weights.astype(jnp.bfloat16), v_win, preferred_element_type=jnp.float32)
            stats.append((top, mass, acc))
        return stats

    local_allowed = (q_index[None, :] <= q_index[:, None]) & (q_seg[None, :] == q_seg[:, None])
    local_stats = stats_of(kv_pair, q_index, local_allowed)
    local_stats, gathered = lax.optimization_barrier((local_stats, gathered))

    c = first_chip + jnp.arange(reach, dtype=jnp.int32)
    slot = ((c // (zs * xs)) * xs + c % xs) * zs + (c // xs) % zs
    kv_window = jnp.take(gathered.reshape(chips, span, -1), slot, axis=0, mode="clip").reshape(window, -1)
    pieces = 2
    piece = window // pieces

    def part(p):
        key_index = start + p * piece + jnp.arange(piece, dtype=jnp.int32)
        k_seg, unused = locate(key_index, lengths)
        allowed = (key_index[None, :] < base) & (k_seg[None, :] == q_seg[:, None])
        return stats_of(kv_window[p * piece : (p + 1) * piece], key_index, allowed)

    all_stats = [local_stats] + [part(p) for p in range(pieces)]

    def attend(m):
        tops = [stats[m][0] for stats in all_stats]
        top = tops[0]
        for other in tops[1:]:
            top = jnp.maximum(top, other)
        acc = 0.0
        mass = 0.0
        for stats in all_stats:
            fade = jnp.exp(stats[m][0] - top)
            mass = mass + stats[m][1] * fade
            acc = acc + stats[m][2] * fade
        return acc / mass

    lam_h = lax.dynamic_index_in_dim(lam, core, keepdims=False)
    gain_h = lax.dynamic_index_in_dim(sub_gain, core, axis=0, keepdims=False)
    diff = attend(0) - lam_h * attend(1)
    head_out = (
        diff * lax.rsqrt(jnp.mean(diff * diff, axis=-1, keepdims=True) + 1e-05) * gain_h * (1.0 - lambda_start)
    ).astype(jnp.bfloat16)
    own_rows = lax.dynamic_slice_in_dim(head_out, core * rows, rows, axis=0)
    other_rows = swap_cores(lax.dynamic_slice_in_dim(head_out, (1 - core) * rows, rows, axis=0))
    merged = jnp.where(
        core == 0,
        jnp.concatenate([own_rows, other_rows], axis=1),
        jnp.concatenate([other_rows, own_rows], axis=1),
    )
    summed = lax.psum(
        jnp.dot(merged, w_out, preferred_element_type=jnp.float32).astype(jnp.bfloat16), "tp"
    ).astype(jnp.float32)
    hidden = (xf + summed).astype(jnp.bfloat16)
    return (hidden, key_flat, values)


def solution(mesh):
    req, tp = mesh.shape["req"], mesh.shape["tp"]
    paired = Mesh(mesh.devices.reshape(req // 16, 2, 4, 2, tp), ("y", "z", "x", "core", "tp"))
    rows = ("y", "z", "x", "core")
    in_specs = (
        P(rows, None),
        P(),
        P(None, "tp"),
        P(None, "tp"),
        P(None, "tp"),
        P("tp", None),
        P(None, "tp", None),
        P("tp", None),
        P(),
    )
    out_specs = (P(rows, None), P(rows, "tp"), P(rows, "tp"))
    return jax.shard_map(
        on_device, mesh=paired, in_specs=in_specs, out_specs=out_specs, check_vma=False
    )
```

```python
import math

import jax
import jax.numpy as jnp
from jax import lax
from jax.sharding import Mesh
from jax.sharding import PartitionSpec as P

QK = 128
VD = 256
MAXLEN = 8192


lambda_start = 0.8 - 0.6 * math.exp(-3.3)
masked_score = -1e30


def locate(index, lengths):
    ends = jnp.cumsum(lengths)
    starts = ends - lengths
    segment = jnp.sum((ends[None, :] <= index[:, None]).astype(jnp.int32), axis=1)
    hit = jnp.arange(lengths.shape[0], dtype=jnp.int32)[None, :] == segment[:, None]
    begin = jnp.sum(jnp.where(hit, starts[None, :], 0), axis=1)
    return (segment, index - begin)


def rotate(proj, position):
    half = proj.shape[-1] // 2
    freq = 10000.0 ** (-jnp.arange(half, dtype=jnp.float32) / half)
    angle = position.astype(jnp.float32)[:, None] * freq[None, :]
    cosine = jnp.cos(angle)[:, None, None, :]
    sine = jnp.sin(angle)[:, None, None, :]
    front = proj[..., :half]
    back = proj[..., half:]
    return jnp.concatenate([front * cosine - back * sine, back * cosine + front * sine], axis=-1)


def swap_cores(value):
    return lax.ppermute(value, "core", [(0, 1), (1, 0)])


def on_device(tokens, norm_gain, w_query, w_key, w_value, w_out, lambdas, sub_gain, lengths):
    rows = tokens.shape[0]
    heads = w_query.shape[1] // (2 * QK)
    key_cols = heads * 2 * QK
    ys, zs, xs = lax.axis_size("y"), lax.axis_size("z"), lax.axis_size("x")
    chips = ys * zs * xs
    total = rows * 2 * chips
    core = lax.axis_index("core")
    chip = (lax.axis_index("y") * zs + lax.axis_index("z")) * xs + lax.axis_index("x")
    first = (chip * 2 + core) * rows
    local_index = first + jnp.arange(rows, dtype=jnp.int32)
    unused, pos_own = locate(local_index, lengths)
    xf = tokens.astype(jnp.float32)
    normed = (xf * lax.rsqrt(jnp.mean(xf * xf, axis=-1, keepdims=True) + 1e-06) * norm_gain).astype(
        jnp.bfloat16
    )
    keys = rotate(
        jnp.dot(normed, w_key, preferred_element_type=jnp.float32).reshape(rows, heads, 2, QK),
        pos_own,
    ).astype(jnp.bfloat16)
    values = jnp.dot(normed, w_value, preferred_element_type=jnp.float32).astype(jnp.bfloat16)
    key_flat = keys.reshape(rows, key_cols)
    lam = (
        jnp.exp(jnp.sum(lambdas[0] * lambdas[1], axis=-1))
        - jnp.exp(jnp.sum(lambdas[2] * lambdas[3], axis=-1))
        + lambda_start
    )
    scale = QK ** (-0.5)

    def head_kv(h):
        k_h = lax.dynamic_index_in_dim(keys, h, axis=1, keepdims=False).reshape(rows, 2 * QK)
        v_h = lax.dynamic_index_in_dim(values.reshape(rows, heads, VD), h, axis=1, keepdims=False)
        return jnp.concatenate([k_h, v_h], axis=1)

    def in_order(mine, theirs, first_is_mine):
        rows_each = mine.shape[0]
        both = jnp.zeros((2 * rows_each,) + mine.shape[1:], mine.dtype)
        both = lax.dynamic_update_slice_in_dim(both, mine, jnp.where(first_is_mine, 0, rows_each), axis=0)
        return lax.dynamic_update_slice_in_dim(both, theirs, jnp.where(first_is_mine, rows_each, 0), axis=0)

    span = 2 * rows
    z = lax.axis_index("z")
    kv_both = jnp.stack([head_kv(0), head_kv(1)], axis=1)
    halves = [lax.ppermute(kv_both[..., i * 2 * QK : (i + 1) * 2 * QK], "z", [(0, 1), (1, 0)]) for i in range(2)]
    kv_chips = in_order(kv_both, jnp.concatenate(halves, axis=-1), z == 0)
    mine = lax.dynamic_index_in_dim(kv_chips, core, axis=1, keepdims=False).reshape(2, rows, -1)
    theirs = swap_cores(lax.dynamic_index_in_dim(kv_chips, 1 - core, axis=1, keepdims=False)).reshape(2, rows, -1)
    quad = jnp.zeros((2, span, mine.shape[-1]), mine.dtype)
    quad = lax.dynamic_update_slice_in_dim(quad, mine, core * rows, axis=1)
    quad = lax.dynamic_update_slice_in_dim(quad, theirs, (1 - core) * rows, axis=1)
    kv_quad = quad.reshape(2 * span, -1)
    kv_pair = lax.dynamic_index_in_dim(quad, z, axis=0, keepdims=False)
    gathered = lax.all_gather(kv_quad, ("y", "x"), axis=0, tiled=True)
    query = rotate(
        jnp.dot(normed, w_query, preferred_element_type=jnp.float32).reshape(rows, heads, 2, QK),
        pos_own,
    ).astype(jnp.bfloat16)
    q_pair = in_order(
        lax.dynamic_index_in_dim(query, core, axis=1, keepdims=False),
        swap_cores(lax.dynamic_index_in_dim(query, 1 - core, axis=1, keepdims=False)),
        core == 0,
    )

    reach = min(MAXLEN // span, chips - 1)
    window = reach * span
    base = chip * span
    first_chip = jnp.clip(chip - reach, 0, chips - reach)
    start = first_chip * span
    q_index = base + jnp.arange(span, dtype=jnp.int32)
    q_seg, unused = locate(q_index, lengths)

    def stats_of(kv_win, key_index, allowed):
        v_win = kv_win[:, 2 * QK :]
        stats = []
        for m in range(2):
            k_m = kv_win[:, m * QK : (m + 1) * QK]
            scores = jnp.einsum("qd,kd->qk", q_pair[:, m, :], k_m, preferred_element_type=jnp.float32) * scale
            scores = jnp.where(allowed, scores, masked_score)
            top = jnp.max(scores, axis=-1, keepdims=True)
            weights = jnp.where(allowed, jnp.exp(scores - top), 0.0)
            mass = jnp.sum(weights, axis=-1, keepdims=True)
            acc = jnp.dot(weights.astype(jnp.bfloat16), v_win, preferred_element_type=jnp.float32)
            stats.append((top, mass, acc))
        return stats

    local_allowed = (q_index[None, :] <= q_index[:, None]) & (q_seg[None, :] == q_seg[:, None])
    local_stats = stats_of(kv_pair, q_index, local_allowed)
    local_stats, gathered = lax.optimization_barrier((local_stats, gathered))

    c = first_chip + jnp.arange(reach, dtype=jnp.int32)
    slot = ((c // (zs * xs)) * xs + c % xs) * zs + (c // xs) % zs
    kv_window = jnp.take(gathered.reshape(chips, span, -1), slot, axis=0, mode="clip").reshape(window, -1)
    pieces = 2
    piece = window // pieces

    def part(p):
        key_index = start + p * piece + jnp.arange(piece, dtype=jnp.int32)
        k_seg, unused = locate(key_index, lengths)
        allowed = (key_index[None, :] < base) & (k_seg[None, :] == q_seg[:, None])
        return stats_of(kv_window[p * piece : (p + 1) * piece], key_index, allowed)

    all_stats = [local_stats] + [part(p) for p in range(pieces)]

    def attend(m):
        tops = [stats[m][0] for stats in all_stats]
        top = tops[0]
        for other in tops[1:]:
            top = jnp.maximum(top, other)
        acc = 0.0
        mass = 0.0
        for stats in all_stats:
            fade = jnp.exp(stats[m][0] - top)
            mass = mass + stats[m][1] * fade
            acc = acc + stats[m][2] * fade
        return acc / mass

    lam_h = lax.dynamic_index_in_dim(lam, core, keepdims=False)
    gain_h = lax.dynamic_index_in_dim(sub_gain, core, axis=0, keepdims=False)
    diff = attend(0) - lam_h * attend(1)
    head_out = (
        diff * lax.rsqrt(jnp.mean(diff * diff, axis=-1, keepdims=True) + 1e-05) * gain_h * (1.0 - lambda_start)
    ).astype(jnp.bfloat16)
    own_rows = lax.dynamic_slice_in_dim(head_out, core * rows, rows, axis=0)
    other_rows = swap_cores(lax.dynamic_slice_in_dim(head_out, (1 - core) * rows, rows, axis=0))
    merged = jnp.where(
        core == 0,
        jnp.concatenate([own_rows, other_rows], axis=1),
        jnp.concatenate([other_rows, own_rows], axis=1),
    )
    summed = lax.psum(
        jnp.dot(merged, w_out, preferred_element_type=jnp.float32).astype(jnp.bfloat16), "tp"
    ).astype(jnp.float32)
    hidden = (xf + summed).astype(jnp.bfloat16)
    return (hidden, key_flat, values)


def solution(mesh):
    req, tp = mesh.shape["req"], mesh.shape["tp"]
    paired = Mesh(mesh.devices.reshape(req // 16, 2, 4, 2, tp), ("y", "z", "x", "core", "tp"))
    rows = ("y", "z", "x", "core")
    in_specs = (
        P(rows, None),
        P(),
        P(None, "tp"),
        P(None, "tp"),
        P(None, "tp"),
        P("tp", None),
        P(None, "tp", None),
        P("tp", None),
        P(),
    )
    out_specs = (P(rows, None), P(rows, "tp"), P(rows, "tp"))
    return jax.shard_map(
        on_device, mesh=paired, in_specs=in_specs, out_specs=out_specs, check_vma=False
    )
```

```python
import math

import jax
import jax.numpy as jnp
from jax import lax
from jax.sharding import Mesh
from jax.sharding import PartitionSpec as P

QK = 128
VD = 256
MAXLEN = 8192


lambda_start = 0.8 - 0.6 * math.exp(-3.3)
masked_score = -1e30


def locate(index, lengths):
    ends = jnp.cumsum(lengths)
    starts = ends - lengths
    segment = jnp.sum((ends[None, :] <= index[:, None]).astype(jnp.int32), axis=1)
    hit = jnp.arange(lengths.shape[0], dtype=jnp.int32)[None, :] == segment[:, None]
    begin = jnp.sum(jnp.where(hit, starts[None, :], 0), axis=1)
    return (segment, index - begin)


def rotate(proj, position):
    half = proj.shape[-1] // 2
    freq = 10000.0 ** (-jnp.arange(half, dtype=jnp.float32) / half)
    angle = position.astype(jnp.float32)[:, None] * freq[None, :]
    cosine = jnp.cos(angle)[:, None, None, :]
    sine = jnp.sin(angle)[:, None, None, :]
    front = proj[..., :half]
    back = proj[..., half:]
    return jnp.concatenate([front * cosine - back * sine, back * cosine + front * sine], axis=-1)


def swap_cores(value):
    return lax.ppermute(value, "core", [(0, 1), (1, 0)])


def on_device(tokens, norm_gain, w_query, w_key, w_value, w_out, lambdas, sub_gain, lengths):
    rows = tokens.shape[0]
    heads = w_query.shape[1] // (2 * QK)
    key_cols = heads * 2 * QK
    ys, zs, xs = lax.axis_size("y"), lax.axis_size("z"), lax.axis_size("x")
    chips = ys * zs * xs
    total = rows * 2 * chips
    core = lax.axis_index("core")
    chip = (lax.axis_index("y") * zs + lax.axis_index("z")) * xs + lax.axis_index("x")
    first = (chip * 2 + core) * rows
    local_index = first + jnp.arange(rows, dtype=jnp.int32)
    unused, pos_own = locate(local_index, lengths)
    xf = tokens.astype(jnp.float32)
    normed = (xf * lax.rsqrt(jnp.mean(xf * xf, axis=-1, keepdims=True) + 1e-06) * norm_gain).astype(
        jnp.bfloat16
    )
    keys = rotate(
        jnp.dot(normed, w_key, preferred_element_type=jnp.float32).reshape(rows, heads, 2, QK),
        pos_own,
    ).astype(jnp.bfloat16)
    values = jnp.dot(normed, w_value, preferred_element_type=jnp.float32).astype(jnp.bfloat16)
    key_flat = keys.reshape(rows, key_cols)
    lam = (
        jnp.exp(jnp.sum(lambdas[0] * lambdas[1], axis=-1))
        - jnp.exp(jnp.sum(lambdas[2] * lambdas[3], axis=-1))
        + lambda_start
    )
    scale = QK ** (-0.5)

    def head_kv(h):
        k_h = lax.dynamic_index_in_dim(keys, h, axis=1, keepdims=False).reshape(rows, 2 * QK)
        v_h = lax.dynamic_index_in_dim(values.reshape(rows, heads, VD), h, axis=1, keepdims=False)
        return jnp.concatenate([k_h, v_h], axis=1)

    def in_order(mine, theirs, first_is_mine):
        rows_each = mine.shape[0]
        both = jnp.zeros((2 * rows_each,) + mine.shape[1:], mine.dtype)
        both = lax.dynamic_update_slice_in_dim(both, mine, jnp.where(first_is_mine, 0, rows_each), axis=0)
        return lax.dynamic_update_slice_in_dim(both, theirs, jnp.where(first_is_mine, rows_each, 0), axis=0)

    span = 2 * rows
    z = lax.axis_index("z")
    kv_both = jnp.stack([head_kv(0), head_kv(1)], axis=1)
    halves = [lax.ppermute(kv_both[..., i * 2 * QK : (i + 1) * 2 * QK], "z", [(0, 1), (1, 0)]) for i in range(2)]
    kv_chips = in_order(kv_both, jnp.concatenate(halves, axis=-1), z == 0)
    mine = lax.dynamic_index_in_dim(kv_chips, core, axis=1, keepdims=False).reshape(2, rows, -1)
    theirs = swap_cores(lax.dynamic_index_in_dim(kv_chips, 1 - core, axis=1, keepdims=False)).reshape(2, rows, -1)
    quad = jnp.zeros((2, span, mine.shape[-1]), mine.dtype)
    quad = lax.dynamic_update_slice_in_dim(quad, mine, core * rows, axis=1)
    quad = lax.dynamic_update_slice_in_dim(quad, theirs, (1 - core) * rows, axis=1)
    kv_quad = quad.reshape(2 * span, -1)
    kv_pair = lax.dynamic_index_in_dim(quad, z, axis=0, keepdims=False)
    gathered = lax.all_gather(kv_quad, ("y", "x"), axis=0, tiled=True)
    query = rotate(
        jnp.dot(normed, w_query, preferred_element_type=jnp.float32).reshape(rows, heads, 2, QK),
        pos_own,
    ).astype(jnp.bfloat16)
    q_pair = in_order(
        lax.dynamic_index_in_dim(query, core, axis=1, keepdims=False),
        swap_cores(lax.dynamic_index_in_dim(query, 1 - core, axis=1, keepdims=False)),
        core == 0,
    )

    reach = min(MAXLEN // span, chips - 1)
    window = reach * span
    base = chip * span
    first_chip = jnp.clip(chip - reach, 0, chips - reach)
    start = first_chip * span
    q_index = base + jnp.arange(span, dtype=jnp.int32)
    q_seg, unused = locate(q_index, lengths)

    def stats_of(kv_win, key_index, allowed):
        v_win = kv_win[:, 2 * QK :]
        stats = []
        for m in range(2):
            k_m = kv_win[:, m * QK : (m + 1) * QK]
            scores = jnp.einsum("qd,kd->qk", q_pair[:, m, :], k_m, preferred_element_type=jnp.float32) * scale
            scores = jnp.where(allowed, scores, masked_score)
            top = jnp.max(scores, axis=-1, keepdims=True)
            weights = jnp.where(allowed, jnp.exp(scores - top), 0.0)
            mass = jnp.sum(weights, axis=-1, keepdims=True)
            acc = jnp.dot(weights.astype(jnp.bfloat16), v_win, preferred_element_type=jnp.float32)
            stats.append((top, mass, acc))
        return stats

    local_allowed = (q_index[None, :] <= q_index[:, None]) & (q_seg[None, :] == q_seg[:, None])
    local_stats = stats_of(kv_pair, q_index, local_allowed)
    local_stats, gathered = lax.optimization_barrier((local_stats, gathered))

    c = first_chip + jnp.arange(reach, dtype=jnp.int32)
    slot = ((c // (zs * xs)) * xs + c % xs) * zs + (c // xs) % zs
    kv_window = jnp.take(gathered.reshape(chips, span, -1), slot, axis=0, mode="clip").reshape(window, -1)
    pieces = 2
    piece = window // pieces

    def part(p):
        key_index = start + p * piece + jnp.arange(piece, dtype=jnp.int32)
        k_seg, unused = locate(key_index, lengths)
        allowed = (key_index[None, :] < base) & (k_seg[None, :] == q_seg[:, None])
        return stats_of(kv_window[p * piece : (p + 1) * piece], key_index, allowed)

    all_stats = [local_stats] + [part(p) for p in range(pieces)]

    def attend(m):
        tops = [stats[m][0] for stats in all_stats]
        top = tops[0]
        for other in tops[1:]:
            top = jnp.maximum(top, other)
        acc = 0.0
        mass = 0.0
        for stats in all_stats:
            fade = jnp.exp(stats[m][0] - top)
            mass = mass + stats[m][1] * fade
            acc = acc + stats[m][2] * fade
        return acc / mass

    lam_h = lax.dynamic_index_in_dim(lam, core, keepdims=False)
    gain_h = lax.dynamic_index_in_dim(sub_gain, core, axis=0, keepdims=False)
    diff = attend(0) - lam_h * attend(1)
    head_out = (
        diff * lax.rsqrt(jnp.mean(diff * diff, axis=-1, keepdims=True) + 1e-05) * gain_h * (1.0 - lambda_start)
    ).astype(jnp.bfloat16)
    own_rows = lax.dynamic_slice_in_dim(head_out, core * rows, rows, axis=0)
    other_rows = swap_cores(lax.dynamic_slice_in_dim(head_out, (1 - core) * rows, rows, axis=0))
    merged = jnp.zeros((rows, 2 * VD), head_out.dtype)
    merged = lax.dynamic_update_slice_in_dim(merged, own_rows, core * VD, axis=1)
    merged = lax.dynamic_update_slice_in_dim(merged, other_rows, (1 - core) * VD, axis=1)
    summed = lax.psum(
        jnp.dot(merged, w_out, preferred_element_type=jnp.float32).astype(jnp.bfloat16), "tp"
    ).astype(jnp.float32)
    hidden = (xf + summed).astype(jnp.bfloat16)
    return (hidden, key_flat, values)


def solution(mesh):
    req, tp = mesh.shape["req"], mesh.shape["tp"]
    paired = Mesh(mesh.devices.reshape(req // 16, 2, 4, 2, tp), ("y", "z", "x", "core", "tp"))
    rows = ("y", "z", "x", "core")
    in_specs = (
        P(rows, None),
        P(),
        P(None, "tp"),
        P(None, "tp"),
        P(None, "tp"),
        P("tp", None),
        P(None, "tp", None),
        P("tp", None),
        P(),
    )
    out_specs = (P(rows, None), P(rows, "tp"), P(rows, "tp"))
    return jax.shard_map(
        on_device, mesh=paired, in_specs=in_specs, out_specs=out_specs, check_vma=False
    )
```
